128 devices in a mesh: row: 8 (over x, core), col: 16 (over z, y).
Axes of the slice: x: 4, y: 4, z: 4, core: 2. Of those that a mesh axis runs over, the one named last changes fastest.
Arguments:
- start_field: float32 [256, 512, 512], P('row', 'col'), may hold values from -6 to 6
- source: float32 [256, 512, 512], P('row', 'col'), may hold values from -9 to 9
- conductance: float32 [256, 512, 512], P('row', 'col'), may hold values from 0.25 to 4
Outputs:
- solution: float32 [256, 512, 512], P('row', 'col')
The draws below stay inside these ranges and needn't reach their ends.
All inputs are finite; a program needn't handle non-finite values.
Results may differ from the reference program's by a relative error of at most 0.00015.
Values sent between devices are 32-bit elements; how exact they have to be, the bound alone decides.
No kernel may reach another device: no remote copies, remote signals or barrier semaphores. Data moves between devices by JAX's collectives and lax.ppermute only.
A program may use at most 128 MiB of HBM per device.

```python
import math
import jax
import jax.numpy as jnp

NZ = 512
NX = 256
NY = 512


mode_list = ((1, 1, 1), (2, 1, 1), (1, 2, 1), (1, 1, 2), (2, 2, 1), (1, 3, 2))


def mode_shape(waves):
    place_x = (jnp.arange(NX, dtype=jnp.float32) + 0.5) / NX
    place_y = (jnp.arange(NY, dtype=jnp.float32) + 0.5) / NY
    place_z = (jnp.arange(NZ, dtype=jnp.float32) + 0.5) / NZ
    along_x = jnp.sin(math.pi * waves[0] * place_x)[:, None, None]
    along_y = jnp.sin(math.pi * waves[1] * place_y)[None, :, None]
    along_z = jnp.sin(math.pi * waves[2] * place_z)[None, None, :]
    return along_x * along_y * along_z


def smooth_modes(key):
    amp_key, sign_key = jax.random.split(key)
    amplitudes = jax.random.uniform(amp_key, (6,), jnp.float32, 0.15, 0.35)
    sign_flip = jnp.where(jax.random.bernoulli(sign_key, 0.5, (6,)), 1.0, -1.0)
    summed = jnp.zeros((NX, NY, NZ), jnp.float32)
    for number in range(6):
        summed = summed + amplitudes[number] * sign_flip[number] * mode_shape(mode_list[number])
    return summed


def draw_source(key, part):
    rough_key, smooth_key = jax.random.split(jax.random.fold_in(key, 11))
    smooth_part = smooth_modes(smooth_key)
    rough_part = jax.random.truncated_normal(rough_key, -5.0, 5.0, (NX, NY, NZ), jnp.float32)
    return rough_part + smooth_part


def levels(rng, dims, pieces, smallest, largest):
    def one(dim, blocks):
        heights = jax.random.uniform(jax.random.fold_in(jax.random.fold_in(rng, 6), dim), (blocks,), jnp.float32, smallest / len(pieces), largest / len(pieces))
        return jnp.repeat(jnp.exp(heights), dims[dim] // blocks).reshape((-1,) + (1,) * (len(dims) - dim - 1))

    level = one(*pieces[0])
    for cut in pieces[1:]:
        level = level * one(*cut)
    return level


def centred(key, shape, scale, limit, pieces=(), kind=jnp.bfloat16):
    array = jax.random.normal(key, shape, jnp.float32) * scale
    if len(pieces) > 0:
        array = levels(key, shape, pieces, -0.22, 0.18) * array
    return jnp.clip(array, min=-limit, max=limit).astype(kind)


def setup_inputs(seed: int = 0) -> dict:
    arg_keys = jax.random.split(jax.random.key(seed), 4)
    start_field = centred(arg_keys[0], (NX, NY, NZ), 1.0, 6.0, ((0, 8), (1, 16)), jnp.float32)
    source = draw_source(jax.random.fold_in(arg_keys[3], 71), 0)
    conductance = jnp.clip(jnp.exp(math.log(4.0) - 2.7725887 * jax.random.uniform(arg_keys[2], (NX, NY, NZ), jnp.float32) ** levels(arg_keys[2], (NX, NY, NZ), ((0, 8), (1, 16)), -0.2, 0.2)), 0.25, 4.0)
    return {"start_field": start_field, "source": source, "conductance": conductance}


damping = 2.0 / 3.0


def face_coefs(conduct, scale):
    padded = jnp.pad(conduct, 1)
    face_x = (padded[1:, 1:-1, 1:-1] + padded[:-1, 1:-1, 1:-1]) * (0.5 * scale)
    face_y = (padded[1:-1, 1:, 1:-1] + padded[1:-1, :-1, 1:-1]) * (0.5 * scale)
    face_z = (padded[1:-1, 1:-1, 1:] + padded[1:-1, 1:-1, :-1]) * (0.5 * scale)
    diagonal = face_x[:-1] + face_x[1:] + face_y[:, :-1] + face_y[:, 1:] + face_z[:, :, :-1] + face_z[:, :, 1:]
    return face_x, face_y, face_z, diagonal


def operate(field, coefs):
    face_x, face_y, face_z, diagonal = coefs
    padded = jnp.pad(field, 1)
    beside = face_x[:-1] * padded[:-2, 1:-1, 1:-1] + face_x[1:] * padded[2:, 1:-1, 1:-1]
    beside = beside + face_y[:, :-1] * padded[1:-1, :-2, 1:-1] + face_y[:, 1:] * padded[1:-1, 2:, 1:-1]
    beside = beside + face_z[:, :, :-1] * padded[1:-1, 1:-1, :-2] + face_z[:, :, 1:] * padded[1:-1, 1:-1, 2:]
    return diagonal * field - beside


def smooth(field, rhs_field, coefs):
    return field + damping * (rhs_field - operate(field, coefs)) / coefs[3]


def restrict_mean(field):
    return field.reshape(field.shape[0] // 2, 2, field.shape[1] // 2, 2, field.shape[2] // 2, 2).mean(axis=(1, 3, 5))


def prolong_copy(field):
    return jnp.repeat(jnp.repeat(jnp.repeat(field, 2, 0), 2, 1), 2, 2)


def reference(start_field, source, conductance):
    fine_co = face_coefs(conductance, 1.0)
    current = start_field
    for sweep_no in range(2):
        current = smooth(current, source, fine_co)
    fine_res = source - operate(current, fine_co)
    mid_cond = restrict_mean(conductance)
    mid_co = face_coefs(mid_cond, 0.25)
    mid_rhs = restrict_mean(fine_res)
    mid_err = damping * mid_rhs / mid_co[3]
    mid_err = smooth(mid_err, mid_rhs, mid_co)
    mid_res = mid_rhs - operate(mid_err, mid_co)
    low_co = face_coefs(restrict_mean(mid_cond), 0.0625)
    low_rhs = restrict_mean(mid_res)
    low_err = damping * low_rhs / low_co[3]
    for sweep_no in range(3):
        low_err = smooth(low_err, low_rhs, low_co)
    mid_err = mid_err + prolong_copy(low_err)
    mid_err = smooth(mid_err, mid_rhs, mid_co)
    current = current + prolong_copy(mid_err)
    for sweep_no in range(2):
        current = smooth(current, source, fine_co)
    return current
```

```python
import jax
import jax.numpy as jnp
from jax import lax
from jax.sharding import PartitionSpec as P

damping = 2.0 / 3.0


def exchange(stack, width):
    for axis, dim in (("row", 1), ("col", 2)):
        count = lax.axis_size(axis)
        forward = [(i, i + 1) for i in range(count - 1)]
        backward = [(i + 1, i) for i in range(count - 1)]
        size = stack.shape[dim]
        low = lax.ppermute(lax.slice_in_dim(stack, size - width, size, axis=dim), axis, forward)
        high = lax.ppermute(lax.slice_in_dim(stack, 0, width, axis=dim), axis, backward)
        stack = jnp.concatenate([low, stack, high], axis=dim)
    return stack


def trim(field, k):
    if k == 0:
        return field
    return field[k:-k, k:-k]


def grid_mask(nx, ny, halo):
    rows = lax.axis_size("row")
    cols = lax.axis_size("col")
    gx = lax.axis_index("row") * nx - halo + lax.broadcasted_iota(jnp.int32, (nx + 2 * halo, 1, 1), 0)
    gy = lax.axis_index("col") * ny - halo + lax.broadcasted_iota(jnp.int32, (1, ny + 2 * halo, 1), 1)
    return ((gx >= 0) & (gx < nx * rows)) & ((gy >= 0) & (gy < ny * cols))


def z_lo(field):
    return jnp.pad(field[:, :, :-1], ((0, 0), (0, 0), (1, 0)))


def z_hi(field):
    return jnp.pad(field[:, :, 1:], ((0, 0), (0, 0), (0, 1)))


def coefs(cond, scale):
    half = 0.5 * scale
    centre = cond[1:-1, 1:-1]
    wxm = (centre + cond[:-2, 1:-1]) * half
    wxp = (cond[2:, 1:-1] + centre) * half
    wym = (centre + cond[1:-1, :-2]) * half
    wyp = (cond[1:-1, 2:] + centre) * half
    wzm = (centre + z_lo(centre)) * half
    wzp = (z_hi(centre) + centre) * half
    diagonal = wxm + wxp + wym + wyp + wzm + wzp
    return wxm, wxp, wym, wyp, wzm, wzp, diagonal


def operate(field, cond, scale):
    wxm, wxp, wym, wyp, wzm, wzp, diagonal = coefs(cond, scale)
    centre = field[1:-1, 1:-1]
    beside = wxm * field[:-2, 1:-1] + wxp * field[2:, 1:-1]
    beside = beside + wym * field[1:-1, :-2] + wyp * field[1:-1, 2:]
    beside = beside + wzm * z_lo(centre) + wzp * z_hi(centre)
    return diagonal * centre - beside, diagonal, centre


def sweep(field, rhs, cond, scale, mask):
    image, diagonal, centre = operate(field, cond, scale)
    return jnp.where(mask, centre + damping * (rhs - image) / diagonal, 0.0)


def first_guess(rhs, cond, scale, mask):
    diagonal = coefs(cond, scale)[6]
    return jnp.where(mask, damping * rhs / diagonal, 0.0)


def restrict_mean(field):
    depth = field.shape[2]
    planar = field.reshape(field.shape[0] // 2, 2, field.shape[1] // 2, 2, depth).sum(axis=(1, 3))
    fine_idx = lax.broadcasted_iota(jnp.int32, (depth, depth // 2), 0)
    coarse_idx = lax.broadcasted_iota(jnp.int32, (depth, depth // 2), 1)
    table = jnp.where(fine_idx // 2 == coarse_idx, 0.125, 0.0).astype(jnp.float32)
    return jnp.dot(
        planar, table, precision=lax.Precision.HIGHEST, preferred_element_type=jnp.float32
    )


def prolong_copy(field):
    depth = field.shape[2]
    coarse_idx = lax.broadcasted_iota(jnp.int32, (depth, 2 * depth), 0)
    fine_idx = lax.broadcasted_iota(jnp.int32, (depth, 2 * depth), 1)
    table = jnp.where(fine_idx // 2 == coarse_idx, 1.0, 0.0).astype(jnp.float32)
    deeper = jnp.dot(
        field, table, precision=lax.Precision.HIGHEST, preferred_element_type=jnp.float32
    )
    return jnp.repeat(jnp.repeat(deeper, 2, 0), 2, 1)


def on_device(start_field, source, conductance):
    nx, ny = start_field.shape[0], start_field.shape[1]
    mx, my = nx // 2, ny // 2
    lx, ly = nx // 4, ny // 4

    with jax.named_scope("level0_down"):
        fine = exchange(jnp.stack([start_field, source, conductance]), 4)
        u0, rhs0, k0 = fine[0], fine[1], fine[2]
        u1 = sweep(u0, trim(rhs0, 1), k0, 1.0, grid_mask(nx, ny, 3))
        u2 = sweep(u1, trim(rhs0, 2), trim(k0, 1), 1.0, grid_mask(nx, ny, 2))
        image = operate(trim(u2, 1), trim(k0, 3), 1.0)[0]
        mid_rhs = restrict_mean(source - image)
        mid_cond = restrict_mean(conductance)

    with jax.named_scope("level1_down"):
        mid = exchange(jnp.stack([mid_rhs, mid_cond]), 4)
        rhs1, k1 = mid[0], mid[1]
        e1 = first_guess(trim(rhs1, 1), k1, 0.25, grid_mask(mx, my, 3))
        e1 = sweep(e1, trim(rhs1, 2), trim(k1, 1), 0.25, grid_mask(mx, my, 2))
        image = operate(trim(e1, 1), trim(k1, 3), 0.25)[0]
        low_rhs = restrict_mean(mid_rhs - image)
        low_cond = restrict_mean(mid_cond)

    with jax.named_scope("level2"):
        low = exchange(jnp.stack([low_rhs, low_cond]), 5)
        rhs2, k2 = low[0], low[1]
        e2 = first_guess(trim(rhs2, 1), k2, 0.0625, grid_mask(lx, ly, 4))
        for halo in (3, 2, 1):
            e2 = sweep(e2, trim(rhs2, 5 - halo), trim(k2, 4 - halo), 0.0625, grid_mask(lx, ly, halo))

    with jax.named_scope("level1_up"):
        e1 = e1 + prolong_copy(e2)
        e1 = sweep(e1, trim(rhs1, 3), trim(k1, 2), 0.25, grid_mask(mx, my, 1))

    with jax.named_scope("level0_up"):
        u3 = u2 + prolong_copy(e1)
        u4 = sweep(u3, trim(rhs0, 3), trim(k0, 2), 1.0, grid_mask(nx, ny, 1))
        u5 = sweep(u4, source, trim(k0, 3), 1.0, grid_mask(nx, ny, 0))
    return u5


def solution(mesh):
    placed = (P("row", "col", None), P("row", "col", None), P("row", "col", None))
    return jax.shard_map(
        on_device, mesh=mesh, in_specs=placed, out_specs=P("row", "col", None), check_vma=False
    )
```

```python
import jax
import jax.numpy as jnp
from jax import lax
from jax.sharding import PartitionSpec as P

damping = 2.0 / 3.0


def exchange(stack, width):
    for axis, dim in (("row", 1), ("col", 2)):
        count = lax.axis_size(axis)
        forward = [(i, i + 1) for i in range(count - 1)]
        backward = [(i + 1, i) for i in range(count - 1)]
        size = stack.shape[dim]
        low = lax.ppermute(lax.slice_in_dim(stack, size - width, size, axis=dim), axis, forward)
        high = lax.ppermute(lax.slice_in_dim(stack, 0, width, axis=dim), axis, backward)
        stack = jnp.concatenate([low, stack, high], axis=dim)
    return stack


def trim(field, k):
    if k == 0:
        return field
    return field[k:-k, k:-k]


def grid_mask(nx, ny, halo):
    rows = lax.axis_size("row")
    cols = lax.axis_size("col")
    gx = lax.axis_index("row") * nx - halo + lax.broadcasted_iota(jnp.int32, (nx + 2 * halo, 1, 1), 0)
    gy = lax.axis_index("col") * ny - halo + lax.broadcasted_iota(jnp.int32, (1, ny + 2 * halo, 1), 1)
    return ((gx >= 0) & (gx < nx * rows)) & ((gy >= 0) & (gy < ny * cols))


def z_lo(field):
    depth_idx = lax.broadcasted_iota(jnp.int32, field.shape, field.ndim - 1)
    return jnp.where(depth_idx == 0, 0.0, jnp.roll(field, 1, field.ndim - 1))


def z_hi(field):
    depth_idx = lax.broadcasted_iota(jnp.int32, field.shape, field.ndim - 1)
    return jnp.where(depth_idx == field.shape[-1] - 1, 0.0, jnp.roll(field, -1, field.ndim - 1))


def coefs(cond, scale):
    half = 0.5 * scale
    centre = cond[1:-1, 1:-1]
    wxm = (centre + cond[:-2, 1:-1]) * half
    wxp = (cond[2:, 1:-1] + centre) * half
    wym = (centre + cond[1:-1, :-2]) * half
    wyp = (cond[1:-1, 2:] + centre) * half
    wzm = (centre + z_lo(centre)) * half
    wzp = (z_hi(centre) + centre) * half
    diagonal = wxm + wxp + wym + wyp + wzm + wzp
    return wxm, wxp, wym, wyp, wzm, wzp, diagonal


def operate(field, cond, scale):
    wxm, wxp, wym, wyp, wzm, wzp, diagonal = coefs(cond, scale)
    centre = field[1:-1, 1:-1]
    beside = wxm * field[:-2, 1:-1] + wxp * field[2:, 1:-1]
    beside = beside + wym * field[1:-1, :-2] + wyp * field[1:-1, 2:]
    beside = beside + wzm * z_lo(centre) + wzp * z_hi(centre)
    return diagonal * centre - beside, diagonal, centre


def sweep(field, rhs, cond, scale, mask):
    image, diagonal, centre = operate(field, cond, scale)
    return jnp.where(mask, centre + damping * (rhs - image) / diagonal, 0.0)


def first_guess(rhs, cond, scale, mask):
    diagonal = coefs(cond, scale)[6]
    return jnp.where(mask, damping * rhs / diagonal, 0.0)


def restrict_mean(field):
    depth = field.shape[2]
    planar = field.reshape(field.shape[0] // 2, 2, field.shape[1] // 2, 2, depth).sum(axis=(1, 3))
    fine_idx = lax.broadcasted_iota(jnp.int32, (depth, depth // 2), 0)
    coarse_idx = lax.broadcasted_iota(jnp.int32, (depth, depth // 2), 1)
    table = jnp.where(fine_idx // 2 == coarse_idx, 0.125, 0.0).astype(jnp.float32)
    return jnp.dot(
        planar, table, precision=lax.Precision.HIGHEST, preferred_element_type=jnp.float32
    )


def prolong_copy(field):
    depth = field.shape[2]
    coarse_idx = lax.broadcasted_iota(jnp.int32, (depth, 2 * depth), 0)
    fine_idx = lax.broadcasted_iota(jnp.int32, (depth, 2 * depth), 1)
    table = jnp.where(fine_idx // 2 == coarse_idx, 1.0, 0.0).astype(jnp.float32)
    deeper = jnp.dot(
        field, table, precision=lax.Precision.HIGHEST, preferred_element_type=jnp.float32
    )
    return jnp.repeat(jnp.repeat(deeper, 2, 0), 2, 1)


def on_device(start_field, source, conductance):
    nx, ny = start_field.shape[0], start_field.shape[1]
    mx, my = nx // 2, ny // 2
    lx, ly = nx // 4, ny // 4

    with jax.named_scope("level0_down"):
        fine = exchange(jnp.stack([start_field, source, conductance]), 4)
        u0, rhs0, k0 = fine[0], fine[1], fine[2]
        u1 = sweep(u0, trim(rhs0, 1), k0, 1.0, grid_mask(nx, ny, 3))
        u2 = sweep(u1, trim(rhs0, 2), trim(k0, 1), 1.0, grid_mask(nx, ny, 2))
        image = operate(trim(u2, 1), trim(k0, 3), 1.0)[0]
        mid_rhs = restrict_mean(source - image)
        mid_cond = restrict_mean(conductance)

    with jax.named_scope("level1_down"):
        mid = exchange(jnp.stack([mid_rhs, mid_cond]), 4)
        rhs1, k1 = mid[0], mid[1]
        e1 = first_guess(trim(rhs1, 1), k1, 0.25, grid_mask(mx, my, 3))
        e1 = sweep(e1, trim(rhs1, 2), trim(k1, 1), 0.25, grid_mask(mx, my, 2))
        image = operate(trim(e1, 1), trim(k1, 3), 0.25)[0]
        low_rhs = restrict_mean(mid_rhs - image)
        low_cond = restrict_mean(mid_cond)

    with jax.named_scope("level2"):
        low = exchange(jnp.stack([low_rhs, low_cond]), 5)
        rhs2, k2 = low[0], low[1]
        e2 = first_guess(trim(rhs2, 1), k2, 0.0625, grid_mask(lx, ly, 4))
        for halo in (3, 2, 1):
            e2 = sweep(e2, trim(rhs2, 5 - halo), trim(k2, 4 - halo), 0.0625, grid_mask(lx, ly, halo))

    with jax.named_scope("level1_up"):
        e1 = e1 + prolong_copy(e2)
        e1 = sweep(e1, trim(rhs1, 3), trim(k1, 2), 0.25, grid_mask(mx, my, 1))

    with jax.named_scope("level0_up"):
        u3 = u2 + prolong_copy(e1)
        u4 = sweep(u3, trim(rhs0, 3), trim(k0, 2), 1.0, grid_mask(nx, ny, 1))
        u5 = sweep(u4, source, trim(k0, 3), 1.0, grid_mask(nx, ny, 0))
    return u5


def solution(mesh):
    placed = (P("row", "col", None), P("row", "col", None), P("row", "col", None))
    return jax.shard_map(
        on_device, mesh=mesh, in_specs=placed, out_specs=P("row", "col", None), check_vma=False
    )
```

```python
import jax
import jax.numpy as jnp
from jax import lax
from jax.sharding import PartitionSpec as P

damping = 2.0 / 3.0


def shifted(block, rows_by, cols_by):
    rows = lax.axis_size("row")
    cols = lax.axis_size("col")
    pairs = []
    for r in range(rows):
        for c in range(cols):
            if 0 <= r + rows_by < rows and 0 <= c + cols_by < cols:
                if cols_by == 0:
                    pairs.append((r, r + rows_by))
                elif rows_by == 0:
                    pairs.append((c, c + cols_by))
                else:
                    pairs.append((r * cols + c, (r + rows_by) * cols + c + cols_by))
    if cols_by == 0:
        return lax.ppermute(block, "row", sorted(set(pairs)))
    if rows_by == 0:
        return lax.ppermute(block, "col", sorted(set(pairs)))
    return lax.ppermute(block, ("row", "col"), pairs)


def exchange(stack, width):
    w = width
    first_x, last_x = stack[:, :w], stack[:, -w:]
    x_lo = shifted(last_x, 1, 0)
    x_hi = shifted(first_x, -1, 0)
    y_lo = shifted(stack[:, :, -w:], 0, 1)
    y_hi = shifted(stack[:, :, :w], 0, -1)
    c_mm = shifted(last_x[:, :, -w:], 1, 1)
    c_mp = shifted(last_x[:, :, :w], 1, -1)
    c_pm = shifted(first_x[:, :, -w:], -1, 1)
    c_pp = shifted(first_x[:, :, :w], -1, -1)
    top = jnp.concatenate([c_mm, x_lo, c_mp], axis=2)
    middle = jnp.concatenate([y_lo, stack, y_hi], axis=2)
    bottom = jnp.concatenate([c_pm, x_hi, c_pp], axis=2)
    return jnp.concatenate([top, middle, bottom], axis=1)


def trim(field, k):
    if k == 0:
        return field
    return field[k:-k, k:-k]


def grid_mask(nx, ny, halo):
    rows = lax.axis_size("row")
    cols = lax.axis_size("col")
    gx = lax.axis_index("row") * nx - halo + lax.broadcasted_iota(jnp.int32, (nx + 2 * halo, 1, 1), 0)
    gy = lax.axis_index("col") * ny - halo + lax.broadcasted_iota(jnp.int32, (1, ny + 2 * halo, 1), 1)
    return ((gx >= 0) & (gx < nx * rows)) & ((gy >= 0) & (gy < ny * cols))


def z_lo(field):
    depth_idx = lax.broadcasted_iota(jnp.int32, field.shape, field.ndim - 1)
    return jnp.where(depth_idx == 0, 0.0, jnp.roll(field, 1, field.ndim - 1))


def z_hi(field):
    depth_idx = lax.broadcasted_iota(jnp.int32, field.shape, field.ndim - 1)
    return jnp.where(depth_idx == field.shape[-1] - 1, 0.0, jnp.roll(field, -1, field.ndim - 1))


def coefs(cond, scale):
    half = 0.5 * scale
    centre = cond[1:-1, 1:-1]
    wxm = (centre + cond[:-2, 1:-1]) * half
    wxp = (cond[2:, 1:-1] + centre) * half
    wym = (centre + cond[1:-1, :-2]) * half
    wyp = (cond[1:-1, 2:] + centre) * half
    wzm = (centre + z_lo(centre)) * half
    wzp = (z_hi(centre) + centre) * half
    diagonal = wxm + wxp + wym + wyp + wzm + wzp
    return wxm, wxp, wym, wyp, wzm, wzp, diagonal


def operate(field, cond, scale):
    wxm, wxp, wym, wyp, wzm, wzp, diagonal = coefs(cond, scale)
    centre = field[1:-1, 1:-1]
    beside = wxm * field[:-2, 1:-1] + wxp * field[2:, 1:-1]
    beside = beside + wym * field[1:-1, :-2] + wyp * field[1:-1, 2:]
    beside = beside + wzm * z_lo(centre) + wzp * z_hi(centre)
    return diagonal * centre - beside, diagonal, centre


def sweep(field, rhs, cond, scale, mask):
    image, diagonal, centre = operate(field, cond, scale)
    return jnp.where(mask, centre + damping * (rhs - image) / diagonal, 0.0)


def first_guess(rhs, cond, scale, mask):
    diagonal = coefs(cond, scale)[6]
    return jnp.where(mask, damping * rhs / diagonal, 0.0)


def restrict_mean(field):
    depth = field.shape[2]
    planar = field.reshape(field.shape[0] // 2, 2, field.shape[1] // 2, 2, depth).sum(axis=(1, 3))
    fine_idx = lax.broadcasted_iota(jnp.int32, (depth, depth // 2), 0)
    coarse_idx = lax.broadcasted_iota(jnp.int32, (depth, depth // 2), 1)
    table = jnp.where(fine_idx // 2 == coarse_idx, 0.125, 0.0).astype(jnp.float32)
    return jnp.dot(
        planar, table, precision=lax.Precision.HIGHEST, preferred_element_type=jnp.float32
    )


def prolong_copy(field):
    depth = field.shape[2]
    coarse_idx = lax.broadcasted_iota(jnp.int32, (depth, 2 * depth), 0)
    fine_idx = lax.broadcasted_iota(jnp.int32, (depth, 2 * depth), 1)
    table = jnp.where(fine_idx // 2 == coarse_idx, 1.0, 0.0).astype(jnp.float32)
    deeper = jnp.dot(
        field, table, precision=lax.Precision.HIGHEST, preferred_element_type=jnp.float32
    )
    return jnp.repeat(jnp.repeat(deeper, 2, 0), 2, 1)


def on_device(start_field, source, conductance):
    nx, ny = start_field.shape[0], start_field.shape[1]
    mx, my = nx // 2, ny // 2
    lx, ly = nx // 4, ny // 4

    with jax.named_scope("level0_down"):
        fine = exchange(jnp.stack([start_field, source, conductance]), 4)
        u0, rhs0, k0 = fine[0], fine[1], fine[2]
        u1 = sweep(u0, trim(rhs0, 1), k0, 1.0, grid_mask(nx, ny, 3))
        u2 = sweep(u1, trim(rhs0, 2), trim(k0, 1), 1.0, grid_mask(nx, ny, 2))
        image = operate(trim(u2, 1), trim(k0, 3), 1.0)[0]
        mid_rhs = restrict_mean(source - image)
        mid_cond = restrict_mean(conductance)

    with jax.named_scope("level1_down"):
        mid = exchange(jnp.stack([mid_rhs, mid_cond]), 4)
        rhs1, k1 = mid[0], mid[1]
        e1 = first_guess(trim(rhs1, 1), k1, 0.25, grid_mask(mx, my, 3))
        e1 = sweep(e1, trim(rhs1, 2), trim(k1, 1), 0.25, grid_mask(mx, my, 2))
        image = operate(trim(e1, 1), trim(k1, 3), 0.25)[0]
        low_rhs = restrict_mean(mid_rhs - image)
        low_cond = restrict_mean(mid_cond)

    with jax.named_scope("level2"):
        low = exchange(jnp.stack([low_rhs, low_cond]), 5)
        rhs2, k2 = low[0], low[1]
        e2 = first_guess(trim(rhs2, 1), k2, 0.0625, grid_mask(lx, ly, 4))
        for halo in (3, 2, 1):
            e2 = sweep(e2, trim(rhs2, 5 - halo), trim(k2, 4 - halo), 0.0625, grid_mask(lx, ly, halo))

    with jax.named_scope("level1_up"):
        e1 = e1 + prolong_copy(e2)
        e1 = sweep(e1, trim(rhs1, 3), trim(k1, 2), 0.25, grid_mask(mx, my, 1))

    with jax.named_scope("level0_up"):
        u3 = u2 + prolong_copy(e1)
        u4 = sweep(u3, trim(rhs0, 3), trim(k0, 2), 1.0, grid_mask(nx, ny, 1))
        u5 = sweep(u4, source, trim(k0, 3), 1.0, grid_mask(nx, ny, 0))
    return u5


def solution(mesh):
    placed = (P("row", "col", None), P("row", "col", None), P("row", "col", None))
    return jax.shard_map(
        on_device, mesh=mesh, in_specs=placed, out_specs=P("row", "col", None), check_vma=False
    )
```

```python
import functools

import jax
import jax.numpy as jnp
from jax import lax
from jax.experimental import pallas as pl
from jax.experimental.pallas import tpu as pltpu
from jax.sharding import PartitionSpec as P

damping = 2.0 / 3.0


def exchange(stack, width):
    for axis, dim in (("row", 1), ("col", 2)):
        count = lax.axis_size(axis)
        forward = [(i, i + 1) for i in range(count - 1)]
        backward = [(i + 1, i) for i in range(count - 1)]
        size = stack.shape[dim]
        low = lax.ppermute(lax.slice_in_dim(stack, size - width, size, axis=dim), axis, forward)
        high = lax.ppermute(lax.slice_in_dim(stack, 0, width, axis=dim), axis, backward)
        stack = jnp.concatenate([low, stack, high], axis=dim)
    return stack


def trim(field, k):
    if k == 0:
        return field
    return field[k:-k, k:-k]


def grid_mask(nx, ny, halo):
    rows = lax.axis_size("row")
    cols = lax.axis_size("col")
    gx = lax.axis_index("row") * nx - halo + lax.broadcasted_iota(jnp.int32, (nx + 2 * halo, 1, 1), 0)
    gy = lax.axis_index("col") * ny - halo + lax.broadcasted_iota(jnp.int32, (1, ny + 2 * halo, 1), 1)
    return ((gx >= 0) & (gx < nx * rows)) & ((gy >= 0) & (gy < ny * cols))


def z_lo(field):
    depth_idx = lax.broadcasted_iota(jnp.int32, field.shape, field.ndim - 1)
    return jnp.where(depth_idx == 0, 0.0, jnp.roll(field, 1, field.ndim - 1))


def z_hi(field):
    depth_idx = lax.broadcasted_iota(jnp.int32, field.shape, field.ndim - 1)
    return jnp.where(depth_idx == field.shape[-1] - 1, 0.0, jnp.roll(field, -1, field.ndim - 1))


def coefs(cond, scale):
    half = 0.5 * scale
    centre = cond[1:-1, 1:-1]
    wxm = (centre + cond[:-2, 1:-1]) * half
    wxp = (cond[2:, 1:-1] + centre) * half
    wym = (centre + cond[1:-1, :-2]) * half
    wyp = (cond[1:-1, 2:] + centre) * half
    wzm = (centre + z_lo(centre)) * half
    wzp = (z_hi(centre) + centre) * half
    diagonal = wxm + wxp + wym + wyp + wzm + wzp
    return wxm, wxp, wym, wyp, wzm, wzp, diagonal


def operate(field, cond, scale):
    wxm, wxp, wym, wyp, wzm, wzp, diagonal = coefs(cond, scale)
    centre = field[1:-1, 1:-1]
    beside = wxm * field[:-2, 1:-1] + wxp * field[2:, 1:-1]
    beside = beside + wym * field[1:-1, :-2] + wyp * field[1:-1, 2:]
    beside = beside + wzm * z_lo(centre) + wzp * z_hi(centre)
    return diagonal * centre - beside, diagonal, centre


def sweep(field, rhs, cond, scale, mask):
    image, diagonal, centre = operate(field, cond, scale)
    return jnp.where(mask, centre + damping * (rhs - image) / diagonal, 0.0)


def first_guess(rhs, cond, scale, mask):
    diagonal = coefs(cond, scale)[6]
    return jnp.where(mask, damping * rhs / diagonal, 0.0)


def restrict_mean(field):
    depth = field.shape[2]
    planar = field.reshape(field.shape[0] // 2, 2, field.shape[1] // 2, 2, depth).sum(axis=(1, 3))
    fine_idx = lax.broadcasted_iota(jnp.int32, (depth, depth // 2), 0)
    coarse_idx = lax.broadcasted_iota(jnp.int32, (depth, depth // 2), 1)
    table = jnp.where(fine_idx // 2 == coarse_idx, 0.125, 0.0).astype(jnp.float32)
    return jnp.dot(
        planar, table, precision=lax.Precision.HIGHEST, preferred_element_type=jnp.float32
    )


def prolong_copy(field):
    depth = field.shape[2]
    coarse_idx = lax.broadcasted_iota(jnp.int32, (depth, 2 * depth), 0)
    fine_idx = lax.broadcasted_iota(jnp.int32, (depth, 2 * depth), 1)
    table = jnp.where(fine_idx // 2 == coarse_idx, 1.0, 0.0).astype(jnp.float32)
    deeper = jnp.dot(
        field, table, precision=lax.Precision.HIGHEST, preferred_element_type=jnp.float32
    )
    return jnp.repeat(jnp.repeat(deeper, 2, 0), 2, 1)


CHUNK = 8


def _plane_kernel(off_ref, u_ref, ulo_ref, uhi_ref, b_ref, k_ref, klo_ref, khi_ref, o_ref, *,
                  scale, extent_x, extent_y, residual):
    step = pl.program_id(0)
    _, depth_y, depth_z = o_ref.shape
    half = 0.5 * scale
    y_idx = lax.broadcasted_iota(jnp.int32, (depth_y, depth_z), 0) + off_ref[1]
    z_idx = lax.broadcasted_iota(jnp.int32, (depth_y, depth_z), 1)
    y_ok = (y_idx >= 0) & (y_idx < extent_y)
    z_first = z_idx == 0
    z_last = z_idx == depth_z - 1

    def y_lo(a):
        return pltpu.roll(a, 1, 0)

    def y_hi(a):
        return pltpu.roll(a, depth_y - 1, 0)

    def z_lo(a):
        return jnp.where(z_first, 0.0, pltpu.roll(a, 1, 1))

    def z_hi(a):
        return jnp.where(z_last, 0.0, pltpu.roll(a, depth_z - 1, 1))

    for p in range(CHUNK):
        km = klo_ref[0] if p == 0 else k_ref[p - 1]
        kp = khi_ref[0] if p == CHUNK - 1 else k_ref[p + 1]
        kc = k_ref[p]
        um = ulo_ref[0] if p == 0 else u_ref[p - 1]
        up = uhi_ref[0] if p == CHUNK - 1 else u_ref[p + 1]
        uc = u_ref[p]
        wxm = (kc + km) * half
        wxp = (kp + kc) * half
        wym = (kc + y_lo(kc)) * half
        wyp = (y_hi(kc) + kc) * half
        wzm = (kc + z_lo(kc)) * half
        wzp = (z_hi(kc) + kc) * half
        diagonal = wxm + wxp + wym + wyp + wzm + wzp
        beside = wxm * um + wxp * up
        beside = beside + wym * y_lo(uc) + wyp * y_hi(uc)
        beside = beside + wzm * z_lo(uc) + wzp * z_hi(uc)
        image = diagonal * uc - beside
        if residual:
            o_ref[p] = b_ref[p] - image
        else:
            x_idx = off_ref[0] + step * CHUNK + p
            ok = y_ok & (x_idx >= 0) & (x_idx < extent_x)
            o_ref[p] = jnp.where(ok, uc + damping * (b_ref[p] - image) / diagonal, 0.0)


def plane_step(offsets, u, b, k, scale, extent_x, extent_y, residual=False):
    (u_arr, u_i), (b_arr, b_i), (k_arr, k_i) = u, b, k
    depth_x, depth_y, depth_z = u_arr.shape[-3:]
    chunks = depth_x // CHUNK

    def spec(arr, idx, kind):
        lead = (None,) if arr.ndim == 4 else ()
        pre = (idx,) if arr.ndim == 4 else ()
        if kind == "main":
            return pl.BlockSpec(lead + (CHUNK, depth_y, depth_z), lambda i, off: pre + (i, 0, 0))
        if kind == "lo":
            return pl.BlockSpec(lead + (1, depth_y, depth_z),
                                lambda i, off: pre + (jnp.maximum(i * CHUNK - 1, 0), 0, 0))
        return pl.BlockSpec(lead + (1, depth_y, depth_z),
                            lambda i, off: pre + (jnp.minimum(i * CHUNK + CHUNK, depth_x - 1), 0, 0))

    kernel = functools.partial(_plane_kernel, scale=scale, extent_x=extent_x,
                               extent_y=extent_y, residual=residual)
    grid_spec = pltpu.PrefetchScalarGridSpec(
        num_scalar_prefetch=1,
        grid=(chunks,),
        in_specs=[spec(u_arr, u_i, "main"), spec(u_arr, u_i, "lo"), spec(u_arr, u_i, "hi"),
                  spec(b_arr, b_i, "main"),
                  spec(k_arr, k_i, "main"), spec(k_arr, k_i, "lo"), spec(k_arr, k_i, "hi")],
        out_specs=pl.BlockSpec((CHUNK, depth_y, depth_z), lambda i, off: (i, 0, 0)),
    )
    cells = depth_x * depth_y * depth_z
    return pl.pallas_call(
        kernel,
        grid_spec=grid_spec,
        out_shape=jax.ShapeDtypeStruct((depth_x, depth_y, depth_z), jnp.float32),
        compiler_params=pltpu.CompilerParams(dimension_semantics=("arbitrary",)),
        cost_estimate=pl.CostEstimate(flops=45 * cells, transcendentals=0, bytes_accessed=4 * 4 * cells),
    )(offsets, u_arr, u_arr, u_arr, b_arr, k_arr, k_arr, k_arr)


def on_device(start_field, source, conductance):
    nx, ny = start_field.shape[0], start_field.shape[1]
    mx, my = nx // 2, ny // 2
    lx, ly = nx // 4, ny // 4

    with jax.named_scope("level0_down"):
        fine = exchange(jnp.stack([start_field, source, conductance]), 4)
        extent_x, extent_y = nx * lax.axis_size("row"), ny * lax.axis_size("col")
        offsets = jnp.stack([lax.axis_index("row") * nx - 4, lax.axis_index("col") * ny - 4]).astype(jnp.int32)
        u1 = plane_step(offsets, (fine, 0), (fine, 1), (fine, 2), 1.0, extent_x, extent_y)
        u2 = plane_step(offsets, (u1, None), (fine, 1), (fine, 2), 1.0, extent_x, extent_y)
        residual = plane_step(offsets, (u2, None), (fine, 1), (fine, 2), 1.0, extent_x, extent_y, residual=True)
        mid_rhs = restrict_mean(trim(residual, 4))
        mid_cond = restrict_mean(conductance)

    with jax.named_scope("level1_down"):
        mid = exchange(jnp.stack([mid_rhs, mid_cond]), 4)
        rhs1, k1 = mid[0], mid[1]
        e1 = first_guess(trim(rhs1, 1), k1, 0.25, grid_mask(mx, my, 3))
        e1 = sweep(e1, trim(rhs1, 2), trim(k1, 1), 0.25, grid_mask(mx, my, 2))
        image = operate(trim(e1, 1), trim(k1, 3), 0.25)[0]
        low_rhs = restrict_mean(mid_rhs - image)
        low_cond = restrict_mean(mid_cond)

    with jax.named_scope("level2"):
        low = exchange(jnp.stack([low_rhs, low_cond]), 5)
        rhs2, k2 = low[0], low[1]
        e2 = first_guess(trim(rhs2, 1), k2, 0.0625, grid_mask(lx, ly, 4))
        for halo in (3, 2, 1):
            e2 = sweep(e2, trim(rhs2, 5 - halo), trim(k2, 4 - halo), 0.0625, grid_mask(lx, ly, halo))

    with jax.named_scope("level1_up"):
        e1 = e1 + prolong_copy(e2)
        e1 = sweep(e1, trim(rhs1, 3), trim(k1, 2), 0.25, grid_mask(mx, my, 1))

    with jax.named_scope("level0_up"):
        u3 = u2 + jnp.pad(prolong_copy(e1), ((2, 2), (2, 2), (0, 0)))
        u4 = plane_step(offsets, (u3, None), (fine, 1), (fine, 2), 1.0, extent_x, extent_y)
        u5 = trim(plane_step(offsets, (u4, None), (fine, 1), (fine, 2), 1.0, extent_x, extent_y), 4)
    return u5


def solution(mesh):
    placed = (P("row", "col", None), P("row", "col", None), P("row", "col", None))
    return jax.shard_map(
        on_device, mesh=mesh, in_specs=placed, out_specs=P("row", "col", None), check_vma=False
    )
```

```python
import functools

import jax
import jax.numpy as jnp
from jax import lax
from jax.experimental import pallas as pl
from jax.experimental.pallas import tpu as pltpu
from jax.sharding import PartitionSpec as P

damping = 2.0 / 3.0


def exchange(stack, width):
    for axis, dim in (("row", 1), ("col", 2)):
        count = lax.axis_size(axis)
        forward = [(i, i + 1) for i in range(count - 1)]
        backward = [(i + 1, i) for i in range(count - 1)]
        size = stack.shape[dim]
        low = lax.ppermute(lax.slice_in_dim(stack, size - width, size, axis=dim), axis, forward)
        high = lax.ppermute(lax.slice_in_dim(stack, 0, width, axis=dim), axis, backward)
        stack = jnp.concatenate([low, stack, high], axis=dim)
    return stack


def trim(field, k):
    if k == 0:
        return field
    return field[k:-k, k:-k]


def grid_mask(nx, ny, halo):
    rows = lax.axis_size("row")
    cols = lax.axis_size("col")
    gx = lax.axis_index("row") * nx - halo + lax.broadcasted_iota(jnp.int32, (nx + 2 * halo, 1, 1), 0)
    gy = lax.axis_index("col") * ny - halo + lax.broadcasted_iota(jnp.int32, (1, ny + 2 * halo, 1), 1)
    return ((gx >= 0) & (gx < nx * rows)) & ((gy >= 0) & (gy < ny * cols))


def z_lo(field):
    depth_idx = lax.broadcasted_iota(jnp.int32, field.shape, field.ndim - 1)
    return jnp.where(depth_idx == 0, 0.0, jnp.roll(field, 1, field.ndim - 1))


def z_hi(field):
    depth_idx = lax.broadcasted_iota(jnp.int32, field.shape, field.ndim - 1)
    return jnp.where(depth_idx == field.shape[-1] - 1, 0.0, jnp.roll(field, -1, field.ndim - 1))


def coefs(cond, scale):
    half = 0.5 * scale
    centre = cond[1:-1, 1:-1]
    wxm = (centre + cond[:-2, 1:-1]) * half
    wxp = (cond[2:, 1:-1] + centre) * half
    wym = (centre + cond[1:-1, :-2]) * half
    wyp = (cond[1:-1, 2:] + centre) * half
    wzm = (centre + z_lo(centre)) * half
    wzp = (z_hi(centre) + centre) * half
    diagonal = wxm + wxp + wym + wyp + wzm + wzp
    return wxm, wxp, wym, wyp, wzm, wzp, diagonal


def operate(field, cond, scale):
    wxm, wxp, wym, wyp, wzm, wzp, diagonal = coefs(cond, scale)
    centre = field[1:-1, 1:-1]
    beside = wxm * field[:-2, 1:-1] + wxp * field[2:, 1:-1]
    beside = beside + wym * field[1:-1, :-2] + wyp * field[1:-1, 2:]
    beside = beside + wzm * z_lo(centre) + wzp * z_hi(centre)
    return diagonal * centre - beside, diagonal, centre


def sweep(field, rhs, cond, scale, mask):
    image, diagonal, centre = operate(field, cond, scale)
    return jnp.where(mask, centre + damping * (rhs - image) / diagonal, 0.0)


def first_guess(rhs, cond, scale, mask):
    diagonal = coefs(cond, scale)[6]
    return jnp.where(mask, damping * rhs / diagonal, 0.0)


def restrict_mean(field):
    depth = field.shape[2]
    planar = field.reshape(field.shape[0] // 2, 2, field.shape[1] // 2, 2, depth).sum(axis=(1, 3))
    fine_idx = lax.broadcasted_iota(jnp.int32, (depth, depth // 2), 0)
    coarse_idx = lax.broadcasted_iota(jnp.int32, (depth, depth // 2), 1)
    table = jnp.where(fine_idx // 2 == coarse_idx, 0.125, 0.0).astype(jnp.float32)
    return jnp.dot(
        planar, table, precision=lax.Precision.HIGHEST, preferred_element_type=jnp.float32
    )


def prolong_copy(field):
    depth = field.shape[2]
    coarse_idx = lax.broadcasted_iota(jnp.int32, (depth, 2 * depth), 0)
    fine_idx = lax.broadcasted_iota(jnp.int32, (depth, 2 * depth), 1)
    table = jnp.where(fine_idx // 2 == coarse_idx, 1.0, 0.0).astype(jnp.float32)
    deeper = jnp.dot(
        field, table, precision=lax.Precision.HIGHEST, preferred_element_type=jnp.float32
    )
    return jnp.repeat(jnp.repeat(deeper, 2, 0), 2, 1)


CHUNK = 8


def _plane_kernel(off_ref, u_ref, ulo_ref, uhi_ref, b_ref, k_ref, klo_ref, khi_ref, o_ref, *,
                  scale, extent_x, extent_y, residual):
    step = pl.program_id(0)
    _, depth_y, depth_z = o_ref.shape
    tiles = depth_y // 8
    half = 0.5 * scale
    z_idx = lax.broadcasted_iota(jnp.int32, (8, depth_z), 1)
    z_first = z_idx == 0
    z_last = z_idx == depth_z - 1
    row_idx = lax.broadcasted_iota(jnp.int32, (8, depth_z), 0)

    def z_lo(a):
        return jnp.where(z_first, 0.0, pltpu.roll(a, 1, 1))

    def z_hi(a):
        return jnp.where(z_last, 0.0, pltpu.roll(a, depth_z - 1, 1))

    def rows(ref, plane, t, shift):
        if shift == 0:
            return ref[plane, pl.ds(8 * t, 8), :]
        if shift < 0 and t == 0:
            return pltpu.roll(ref[plane, pl.ds(0, 8), :], 1, 0)
        if shift > 0 and t == tiles - 1:
            return pltpu.roll(ref[plane, pl.ds(8 * t, 8), :], 7, 0)
        return ref[plane, pl.ds(8 * t + shift, 8), :]

    for p in range(CHUNK):
        k_m = (klo_ref, 0) if p == 0 else (k_ref, p - 1)
        k_p = (khi_ref, 0) if p == CHUNK - 1 else (k_ref, p + 1)
        u_m = (ulo_ref, 0) if p == 0 else (u_ref, p - 1)
        u_p = (uhi_ref, 0) if p == CHUNK - 1 else (u_ref, p + 1)
        x_idx = off_ref[0] + step * CHUNK + p
        x_ok = (x_idx >= 0) & (x_idx < extent_x)
        for t in range(tiles):
            kc = rows(k_ref, p, t, 0)
            uc = rows(u_ref, p, t, 0)
            sxm = kc + rows(k_m[0], k_m[1], t, 0)
            sxp = rows(k_p[0], k_p[1], t, 0) + kc
            sym = kc + rows(k_ref, p, t, -1)
            syp = rows(k_ref, p, t, 1) + kc
            szm = kc + z_lo(kc)
            szp = z_hi(kc) + kc
            total = sxm + sxp + sym + syp + szm + szp
            beside = sxm * rows(u_m[0], u_m[1], t, 0) + sxp * rows(u_p[0], u_p[1], t, 0)
            beside = beside + sym * rows(u_ref, p, t, -1) + syp * rows(u_ref, p, t, 1)
            beside = beside + szm * z_lo(uc) + szp * z_hi(uc)
            image = (total * uc - beside) * half
            if residual:
                o_ref[p, pl.ds(8 * t, 8), :] = b_ref[p, pl.ds(8 * t, 8), :] - image
            else:
                y_idx = off_ref[1] + 8 * t + row_idx
                ok = x_ok & (y_idx >= 0) & (y_idx < extent_y)
                fresh = uc + damping * (b_ref[p, pl.ds(8 * t, 8), :] - image) / (total * half)
                o_ref[p, pl.ds(8 * t, 8), :] = jnp.where(ok, fresh, 0.0)


def plane_step(offsets, u, b, k, scale, extent_x, extent_y, residual=False):
    (u_arr, u_i), (b_arr, b_i), (k_arr, k_i) = u, b, k
    depth_x, depth_y, depth_z = u_arr.shape[-3:]
    chunks = depth_x // CHUNK

    def spec(arr, idx, kind):
        lead = (None,) if arr.ndim == 4 else ()
        pre = (idx,) if arr.ndim == 4 else ()
        if kind == "main":
            return pl.BlockSpec(lead + (CHUNK, depth_y, depth_z), lambda i, off: pre + (i, 0, 0))
        if kind == "lo":
            return pl.BlockSpec(lead + (1, depth_y, depth_z),
                                lambda i, off: pre + (jnp.maximum(i * CHUNK - 1, 0), 0, 0))
        return pl.BlockSpec(lead + (1, depth_y, depth_z),
                            lambda i, off: pre + (jnp.minimum(i * CHUNK + CHUNK, depth_x - 1), 0, 0))

    kernel = functools.partial(_plane_kernel, scale=scale, extent_x=extent_x,
                               extent_y=extent_y, residual=residual)
    grid_spec = pltpu.PrefetchScalarGridSpec(
        num_scalar_prefetch=1,
        grid=(chunks,),
        in_specs=[spec(u_arr, u_i, "main"), spec(u_arr, u_i, "lo"), spec(u_arr, u_i, "hi"),
                  spec(b_arr, b_i, "main"),
                  spec(k_arr, k_i, "main"), spec(k_arr, k_i, "lo"), spec(k_arr, k_i, "hi")],
        out_specs=pl.BlockSpec((CHUNK, depth_y, depth_z), lambda i, off: (i, 0, 0)),
    )
    cells = depth_x * depth_y * depth_z
    return pl.pallas_call(
        kernel,
        grid_spec=grid_spec,
        out_shape=jax.ShapeDtypeStruct((depth_x, depth_y, depth_z), jnp.float32),
        compiler_params=pltpu.CompilerParams(dimension_semantics=("arbitrary",)),
        cost_estimate=pl.CostEstimate(flops=45 * cells, transcendentals=0, bytes_accessed=4 * 4 * cells),
    )(offsets, u_arr, u_arr, u_arr, b_arr, k_arr, k_arr, k_arr)


def on_device(start_field, source, conductance):
    nx, ny = start_field.shape[0], start_field.shape[1]
    mx, my = nx // 2, ny // 2
    lx, ly = nx // 4, ny // 4

    with jax.named_scope("level0_down"):
        fine = exchange(jnp.stack([start_field, source, conductance]), 4)
        extent_x, extent_y = nx * lax.axis_size("row"), ny * lax.axis_size("col")
        offsets = jnp.stack([lax.axis_index("row") * nx - 4, lax.axis_index("col") * ny - 4]).astype(jnp.int32)
        u1 = plane_step(offsets, (fine, 0), (fine, 1), (fine, 2), 1.0, extent_x, extent_y)
        u2 = plane_step(offsets, (u1, None), (fine, 1), (fine, 2), 1.0, extent_x, extent_y)
        residual = plane_step(offsets, (u2, None), (fine, 1), (fine, 2), 1.0, extent_x, extent_y, residual=True)
        mid_rhs = restrict_mean(trim(residual, 4))
        mid_cond = restrict_mean(conductance)

    with jax.named_scope("level1_down"):
        mid = exchange(jnp.stack([mid_rhs, mid_cond]), 4)
        rhs1, k1 = mid[0], mid[1]
        e1 = first_guess(trim(rhs1, 1), k1, 0.25, grid_mask(mx, my, 3))
        e1 = sweep(e1, trim(rhs1, 2), trim(k1, 1), 0.25, grid_mask(mx, my, 2))
        image = operate(trim(e1, 1), trim(k1, 3), 0.25)[0]
        low_rhs = restrict_mean(mid_rhs - image)
        low_cond = restrict_mean(mid_cond)

    with jax.named_scope("level2"):
        low = exchange(jnp.stack([low_rhs, low_cond]), 5)
        rhs2, k2 = low[0], low[1]
        e2 = first_guess(trim(rhs2, 1), k2, 0.0625, grid_mask(lx, ly, 4))
        for halo in (3, 2, 1):
            e2 = sweep(e2, trim(rhs2, 5 - halo), trim(k2, 4 - halo), 0.0625, grid_mask(lx, ly, halo))

    with jax.named_scope("level1_up"):
        e1 = e1 + prolong_copy(e2)
        e1 = sweep(e1, trim(rhs1, 3), trim(k1, 2), 0.25, grid_mask(mx, my, 1))

    with jax.named_scope("level0_up"):
        u3 = u2 + jnp.pad(prolong_copy(e1), ((2, 2), (2, 2), (0, 0)))
        u4 = plane_step(offsets, (u3, None), (fine, 1), (fine, 2), 1.0, extent_x, extent_y)
        u5 = trim(plane_step(offsets, (u4, None), (fine, 1), (fine, 2), 1.0, extent_x, extent_y), 4)
    return u5


def solution(mesh):
    placed = (P("row", "col", None), P("row", "col", None), P("row", "col", None))
    return jax.shard_map(
        on_device, mesh=mesh, in_specs=placed, out_specs=P("row", "col", None), check_vma=False
    )
```

```python
import functools

import jax
import jax.numpy as jnp
from jax import lax
from jax.experimental import pallas as pl
from jax.experimental.pallas import tpu as pltpu
from jax.sharding import PartitionSpec as P

damping = 2.0 / 3.0


def exchange(stack, width):
    for axis, dim in (("row", 1), ("col", 2)):
        count = lax.axis_size(axis)
        forward = [(i, i + 1) for i in range(count - 1)]
        backward = [(i + 1, i) for i in range(count - 1)]
        size = stack.shape[dim]
        low = lax.ppermute(lax.slice_in_dim(stack, size - width, size, axis=dim), axis, forward)
        high = lax.ppermute(lax.slice_in_dim(stack, 0, width, axis=dim), axis, backward)
        stack = jnp.concatenate([low, stack, high], axis=dim)
    return stack


def trim(field, k):
    if k == 0:
        return field
    return field[k:-k, k:-k]


def grid_mask(nx, ny, halo):
    rows = lax.axis_size("row")
    cols = lax.axis_size("col")
    gx = lax.axis_index("row") * nx - halo + lax.broadcasted_iota(jnp.int32, (nx + 2 * halo, 1, 1), 0)
    gy = lax.axis_index("col") * ny - halo + lax.broadcasted_iota(jnp.int32, (1, ny + 2 * halo, 1), 1)
    return ((gx >= 0) & (gx < nx * rows)) & ((gy >= 0) & (gy < ny * cols))


def z_lo(field):
    depth_idx = lax.broadcasted_iota(jnp.int32, field.shape, field.ndim - 1)
    return jnp.where(depth_idx == 0, 0.0, jnp.roll(field, 1, field.ndim - 1))


def z_hi(field):
    depth_idx = lax.broadcasted_iota(jnp.int32, field.shape, field.ndim - 1)
    return jnp.where(depth_idx == field.shape[-1] - 1, 0.0, jnp.roll(field, -1, field.ndim - 1))


def coefs(cond, scale):
    half = 0.5 * scale
    centre = cond[1:-1, 1:-1]
    wxm = (centre + cond[:-2, 1:-1]) * half
    wxp = (cond[2:, 1:-1] + centre) * half
    wym = (centre + cond[1:-1, :-2]) * half
    wyp = (cond[1:-1, 2:] + centre) * half
    wzm = (centre + z_lo(centre)) * half
    wzp = (z_hi(centre) + centre) * half
    diagonal = wxm + wxp + wym + wyp + wzm + wzp
    return wxm, wxp, wym, wyp, wzm, wzp, diagonal


def operate(field, cond, scale):
    wxm, wxp, wym, wyp, wzm, wzp, diagonal = coefs(cond, scale)
    centre = field[1:-1, 1:-1]
    beside = wxm * field[:-2, 1:-1] + wxp * field[2:, 1:-1]
    beside = beside + wym * field[1:-1, :-2] + wyp * field[1:-1, 2:]
    beside = beside + wzm * z_lo(centre) + wzp * z_hi(centre)
    return diagonal * centre - beside, diagonal, centre


def sweep(field, rhs, cond, scale, mask):
    image, diagonal, centre = operate(field, cond, scale)
    return jnp.where(mask, centre + damping * (rhs - image) / diagonal, 0.0)


def first_guess(rhs, cond, scale, mask):
    diagonal = coefs(cond, scale)[6]
    return jnp.where(mask, damping * rhs / diagonal, 0.0)


def restrict_mean(field):
    depth = field.shape[2]
    planar = field.reshape(field.shape[0] // 2, 2, field.shape[1] // 2, 2, depth).sum(axis=(1, 3))
    fine_idx = lax.broadcasted_iota(jnp.int32, (depth, depth // 2), 0)
    coarse_idx = lax.broadcasted_iota(jnp.int32, (depth, depth // 2), 1)
    table = jnp.where(fine_idx // 2 == coarse_idx, 0.125, 0.0).astype(jnp.float32)
    return jnp.dot(
        planar, table, precision=lax.Precision.HIGHEST, preferred_element_type=jnp.float32
    )


def prolong_copy(field):
    depth = field.shape[2]
    coarse_idx = lax.broadcasted_iota(jnp.int32, (depth, 2 * depth), 0)
    fine_idx = lax.broadcasted_iota(jnp.int32, (depth, 2 * depth), 1)
    table = jnp.where(fine_idx // 2 == coarse_idx, 1.0, 0.0).astype(jnp.float32)
    deeper = jnp.dot(
        field, table, precision=lax.Precision.HIGHEST, preferred_element_type=jnp.float32
    )
    return jnp.repeat(jnp.repeat(deeper, 2, 0), 2, 1)


CHUNK = 8


def _plane_kernel(off_ref, u_ref, ulo_ref, uhi_ref, b_ref, k_ref, klo_ref, khi_ref, o_ref, *,
                  scale, extent_x, extent_y, residual, chunk, inner):
    step = pl.program_id(0)
    depth_y, depth_z = u_ref.shape[-2], u_ref.shape[-1]
    first = 4 if inner else 0
    tiles = (depth_y - 2 * first) // 8
    half = 0.5 * scale
    z_idx = lax.broadcasted_iota(jnp.int32, (8, depth_z), 1)
    z_first = z_idx == 0
    z_last = z_idx == depth_z - 1
    row_idx = lax.broadcasted_iota(jnp.int32, (8, depth_z), 0)

    def z_lo(a):
        return jnp.where(z_first, 0.0, pltpu.roll(a, 1, 1))

    def z_hi(a):
        return jnp.where(z_last, 0.0, pltpu.roll(a, depth_z - 1, 1))

    def rows(ref, plane, t, shift):
        start = first + 8 * t
        if shift == 0:
            return ref[plane, pl.ds(start, 8), :]
        if shift < 0 and start == 0:
            return pltpu.roll(ref[plane, pl.ds(0, 8), :], 1, 0)
        if shift > 0 and start + 8 == depth_y:
            return pltpu.roll(ref[plane, pl.ds(start, 8), :], 7, 0)
        return ref[plane, pl.ds(start + shift, 8), :]

    for p in range(chunk):
        k_m = (klo_ref, 0) if p == 0 else (k_ref, p - 1)
        k_p = (khi_ref, 0) if p == chunk - 1 else (k_ref, p + 1)
        u_m = (ulo_ref, 0) if p == 0 else (u_ref, p - 1)
        u_p = (uhi_ref, 0) if p == chunk - 1 else (u_ref, p + 1)
        x_idx = off_ref[0] + first + step * chunk + p
        x_ok = (x_idx >= 0) & (x_idx < extent_x)
        for t in range(tiles):
            kc = rows(k_ref, p, t, 0)
            uc = rows(u_ref, p, t, 0)
            sxm = kc + rows(k_m[0], k_m[1], t, 0)
            sxp = rows(k_p[0], k_p[1], t, 0) + kc
            sym = kc + rows(k_ref, p, t, -1)
            syp = rows(k_ref, p, t, 1) + kc
            szm = kc + z_lo(kc)
            szp = z_hi(kc) + kc
            total = sxm + sxp + sym + syp + szm + szp
            beside = sxm * rows(u_m[0], u_m[1], t, 0) + sxp * rows(u_p[0], u_p[1], t, 0)
            beside = beside + sym * rows(u_ref, p, t, -1) + syp * rows(u_ref, p, t, 1)
            beside = beside + szm * z_lo(uc) + szp * z_hi(uc)
            image = (total * uc - beside) * half
            rhs = rows(b_ref, p, t, 0)
            out_rows = pl.ds(8 * t if inner else first + 8 * t, 8)
            if residual:
                o_ref[p, out_rows, :] = rhs - image
            else:
                y_idx = off_ref[1] + first + 8 * t + row_idx
                ok = x_ok & (y_idx >= 0) & (y_idx < extent_y)
                fresh = uc + damping * (rhs - image) / (total * half)
                o_ref[p, out_rows, :] = jnp.where(ok, fresh, 0.0)


def plane_step(offsets, u, b, k, scale, extent_x, extent_y, residual=False, inner=False):
    (u_arr, u_i), (b_arr, b_i), (k_arr, k_i) = u, b, k
    depth_x, depth_y, depth_z = u_arr.shape[-3:]
    chunk = 4 if inner else CHUNK
    lead_blocks = 1 if inner else 0
    chunks = (depth_x - 8 * lead_blocks) // chunk

    def spec(arr, idx, kind):
        lead = (None,) if arr.ndim == 4 else ()
        pre = (idx,) if arr.ndim == 4 else ()
        if kind == "main":
            return pl.BlockSpec(lead + (chunk, depth_y, depth_z),
                                lambda i, off: pre + (i + lead_blocks, 0, 0))
        if kind == "lo":
            return pl.BlockSpec(lead + (1, depth_y, depth_z),
                                lambda i, off: pre + (jnp.maximum((i + lead_blocks) * chunk - 1, 0), 0, 0))
        return pl.BlockSpec(lead + (1, depth_y, depth_z),
                            lambda i, off: pre + (jnp.minimum((i + lead_blocks) * chunk + chunk, depth_x - 1), 0, 0))

    kernel = functools.partial(_plane_kernel, scale=scale, extent_x=extent_x, extent_y=extent_y,
                               residual=residual, chunk=chunk, inner=inner)
    out_x = depth_x - 8 if inner else depth_x
    out_y = depth_y - 8 if inner else depth_y
    grid_spec = pltpu.PrefetchScalarGridSpec(
        num_scalar_prefetch=1,
        grid=(chunks,),
        in_specs=[spec(u_arr, u_i, "main"), spec(u_arr, u_i, "lo"), spec(u_arr, u_i, "hi"),
                  spec(b_arr, b_i, "main"),
                  spec(k_arr, k_i, "main"), spec(k_arr, k_i, "lo"), spec(k_arr, k_i, "hi")],
        out_specs=pl.BlockSpec((chunk, out_y, depth_z), lambda i, off: (i, 0, 0)),
    )
    cells = out_x * out_y * depth_z
    return pl.pallas_call(
        kernel,
        grid_spec=grid_spec,
        out_shape=jax.ShapeDtypeStruct((out_x, out_y, depth_z), jnp.float32),
        compiler_params=pltpu.CompilerParams(dimension_semantics=("arbitrary",)),
        cost_estimate=pl.CostEstimate(flops=45 * cells, transcendentals=0, bytes_accessed=4 * 4 * cells),
    )(offsets, u_arr, u_arr, u_arr, b_arr, k_arr, k_arr, k_arr)


def on_device(start_field, source, conductance):
    nx, ny = start_field.shape[0], start_field.shape[1]
    mx, my = nx // 2, ny // 2
    lx, ly = nx // 4, ny // 4

    with jax.named_scope("level0_down"):
        fine = exchange(jnp.stack([start_field, source, conductance]), 4)
        extent_x, extent_y = nx * lax.axis_size("row"), ny * lax.axis_size("col")
        offsets = jnp.stack([lax.axis_index("row") * nx - 4, lax.axis_index("col") * ny - 4]).astype(jnp.int32)
        u1 = plane_step(offsets, (fine, 0), (fine, 1), (fine, 2), 1.0, extent_x, extent_y)
        u2 = plane_step(offsets, (u1, None), (fine, 1), (fine, 2), 1.0, extent_x, extent_y)
        residual = plane_step(offsets, (u2, None), (fine, 1), (fine, 2), 1.0, extent_x, extent_y,
                              residual=True, inner=True)
        mid_rhs = restrict_mean(residual)
        mid_cond = restrict_mean(conductance)

    with jax.named_scope("level1_down"):
        mid = exchange(jnp.stack([mid_rhs, mid_cond]), 4)
        rhs1, k1 = mid[0], mid[1]
        e1 = first_guess(trim(rhs1, 1), k1, 0.25, grid_mask(mx, my, 3))
        e1 = sweep(e1, trim(rhs1, 2), trim(k1, 1), 0.25, grid_mask(mx, my, 2))
        image = operate(trim(e1, 1), trim(k1, 3), 0.25)[0]
        low_rhs = restrict_mean(mid_rhs - image)
        low_cond = restrict_mean(mid_cond)

    with jax.named_scope("level2"):
        low = exchange(jnp.stack([low_rhs, low_cond]), 5)
        rhs2, k2 = low[0], low[1]
        e2 = first_guess(trim(rhs2, 1), k2, 0.0625, grid_mask(lx, ly, 4))
        for halo in (3, 2, 1):
            e2 = sweep(e2, trim(rhs2, 5 - halo), trim(k2, 4 - halo), 0.0625, grid_mask(lx, ly, halo))

    with jax.named_scope("level1_up"):
        e1 = e1 + prolong_copy(e2)
        e1 = sweep(e1, trim(rhs1, 3), trim(k1, 2), 0.25, grid_mask(mx, my, 1))

    with jax.named_scope("level0_up"):
        u3 = u2 + jnp.pad(prolong_copy(e1), ((2, 2), (2, 2), (0, 0)))
        u4 = plane_step(offsets, (u3, None), (fine, 1), (fine, 2), 1.0, extent_x, extent_y)
        u5 = plane_step(offsets, (u4, None), (fine, 1), (fine, 2), 1.0, extent_x, extent_y, inner=True)
    return u5


def solution(mesh):
    placed = (P("row", "col", None), P("row", "col", None), P("row", "col", None))
    return jax.shard_map(
        on_device, mesh=mesh, in_specs=placed, out_specs=P("row", "col", None), check_vma=False
    )
```

```python
import functools

import jax
import jax.numpy as jnp
from jax import lax
from jax.experimental import pallas as pl
from jax.experimental.pallas import tpu as pltpu
from jax.sharding import PartitionSpec as P

damping = 2.0 / 3.0


def exchange(stack, width):
    for axis, dim in (("row", 1), ("col", 2)):
        count = lax.axis_size(axis)
        forward = [(i, i + 1) for i in range(count - 1)]
        backward = [(i + 1, i) for i in range(count - 1)]
        size = stack.shape[dim]
        low = lax.ppermute(lax.slice_in_dim(stack, size - width, size, axis=dim), axis, forward)
        high = lax.ppermute(lax.slice_in_dim(stack, 0, width, axis=dim), axis, backward)
        stack = jnp.concatenate([low, stack, high], axis=dim)
    return stack


def trim(field, k):
    if k == 0:
        return field
    return field[k:-k, k:-k]


def grid_mask(nx, ny, halo):
    rows = lax.axis_size("row")
    cols = lax.axis_size("col")
    gx = lax.axis_index("row") * nx - halo + lax.broadcasted_iota(jnp.int32, (nx + 2 * halo, 1, 1), 0)
    gy = lax.axis_index("col") * ny - halo + lax.broadcasted_iota(jnp.int32, (1, ny + 2 * halo, 1), 1)
    return ((gx >= 0) & (gx < nx * rows)) & ((gy >= 0) & (gy < ny * cols))


def z_lo(field):
    depth_idx = lax.broadcasted_iota(jnp.int32, field.shape, field.ndim - 1)
    return jnp.where(depth_idx == 0, 0.0, jnp.roll(field, 1, field.ndim - 1))


def z_hi(field):
    depth_idx = lax.broadcasted_iota(jnp.int32, field.shape, field.ndim - 1)
    return jnp.where(depth_idx == field.shape[-1] - 1, 0.0, jnp.roll(field, -1, field.ndim - 1))


def coefs(cond, scale):
    half = 0.5 * scale
    centre = cond[1:-1, 1:-1]
    wxm = (centre + cond[:-2, 1:-1]) * half
    wxp = (cond[2:, 1:-1] + centre) * half
    wym = (centre + cond[1:-1, :-2]) * half
    wyp = (cond[1:-1, 2:] + centre) * half
    wzm = (centre + z_lo(centre)) * half
    wzp = (z_hi(centre) + centre) * half
    diagonal = wxm + wxp + wym + wyp + wzm + wzp
    return wxm, wxp, wym, wyp, wzm, wzp, diagonal


def operate(field, cond, scale):
    wxm, wxp, wym, wyp, wzm, wzp, diagonal = coefs(cond, scale)
    centre = field[1:-1, 1:-1]
    beside = wxm * field[:-2, 1:-1] + wxp * field[2:, 1:-1]
    beside = beside + wym * field[1:-1, :-2] + wyp * field[1:-1, 2:]
    beside = beside + wzm * z_lo(centre) + wzp * z_hi(centre)
    return diagonal * centre - beside, diagonal, centre


def sweep(field, rhs, cond, scale, mask):
    image, diagonal, centre = operate(field, cond, scale)
    return jnp.where(mask, centre + damping * (rhs - image) / diagonal, 0.0)


def first_guess(rhs, cond, scale, mask):
    diagonal = coefs(cond, scale)[6]
    return jnp.where(mask, damping * rhs / diagonal, 0.0)


def restrict_mean(field):
    depth = field.shape[2]
    planar = field.reshape(field.shape[0] // 2, 2, field.shape[1] // 2, 2, depth).sum(axis=(1, 3))
    fine_idx = lax.broadcasted_iota(jnp.int32, (depth, depth // 2), 0)
    coarse_idx = lax.broadcasted_iota(jnp.int32, (depth, depth // 2), 1)
    table = jnp.where(fine_idx // 2 == coarse_idx, 0.125, 0.0).astype(jnp.float32)
    return jnp.dot(
        planar, table, precision=lax.Precision.HIGHEST, preferred_element_type=jnp.float32
    )


def prolong_copy(field):
    depth = field.shape[2]
    coarse_idx = lax.broadcasted_iota(jnp.int32, (depth, 2 * depth), 0)
    fine_idx = lax.broadcasted_iota(jnp.int32, (depth, 2 * depth), 1)
    table = jnp.where(fine_idx // 2 == coarse_idx, 1.0, 0.0).astype(jnp.float32)
    deeper = jnp.dot(
        field, table, precision=lax.Precision.HIGHEST, preferred_element_type=jnp.float32
    )
    return jnp.repeat(jnp.repeat(deeper, 2, 0), 2, 1)


CHUNK = 8


def _plane_kernel(off_ref, u_ref, ulo_ref, uhi_ref, b_ref, k_ref, klo_ref, khi_ref, o_ref, *,
                  scale, extent_x, extent_y, residual, chunk, inner):
    step = pl.program_id(0)
    depth_y, depth_z = u_ref.shape[-2], u_ref.shape[-1]
    first = 4 if inner else 0
    tiles = (depth_y - 2 * first) // 8
    half = 0.5 * scale
    z_idx = lax.broadcasted_iota(jnp.int32, (8, depth_z), 1)
    z_first = z_idx == 0
    z_last = z_idx == depth_z - 1
    row_idx = lax.broadcasted_iota(jnp.int32, (8, depth_z), 0)

    def z_lo(a):
        return jnp.where(z_first, 0.0, pltpu.roll(a, 1, 1))

    def z_hi(a):
        return jnp.where(z_last, 0.0, pltpu.roll(a, depth_z - 1, 1))

    def rows(ref, plane, t, shift):
        start = first + 8 * t
        if shift == 0:
            return ref[plane, pl.ds(start, 8), :]
        if shift < 0 and start == 0:
            return pltpu.roll(ref[plane, pl.ds(0, 8), :], 1, 0)
        if shift > 0 and start + 8 == depth_y:
            return pltpu.roll(ref[plane, pl.ds(start, 8), :], 7, 0)
        return ref[plane, pl.ds(start + shift, 8), :]

    for p in range(chunk):
        k_m = (klo_ref, 0) if p == 0 else (k_ref, p - 1)
        k_p = (khi_ref, 0) if p == chunk - 1 else (k_ref, p + 1)
        u_m = (ulo_ref, 0) if p == 0 else (u_ref, p - 1)
        u_p = (uhi_ref, 0) if p == chunk - 1 else (u_ref, p + 1)
        x_idx = off_ref[0] + first + step * chunk + p
        x_ok = (x_idx >= 0) & (x_idx < extent_x)
        for t in range(tiles):
            kc = rows(k_ref, p, t, 0)
            uc = rows(u_ref, p, t, 0)
            sxm = kc + rows(k_m[0], k_m[1], t, 0)
            sxp = rows(k_p[0], k_p[1], t, 0) + kc
            sym = kc + rows(k_ref, p, t, -1)
            syp = rows(k_ref, p, t, 1) + kc
            szm = kc + z_lo(kc)
            szp = z_hi(kc) + kc
            total = sxm + sxp + sym + syp + szm + szp
            beside = sxm * rows(u_m[0], u_m[1], t, 0) + sxp * rows(u_p[0], u_p[1], t, 0)
            beside = beside + sym * rows(u_ref, p, t, -1) + syp * rows(u_ref, p, t, 1)
            beside = beside + szm * z_lo(uc) + szp * z_hi(uc)
            image = (total * uc - beside) * half
            rhs = rows(b_ref, p, t, 0)
            out_rows = pl.ds(8 * t if inner else first + 8 * t, 8)
            if residual:
                o_ref[p, out_rows, :] = rhs - image
            else:
                y_idx = off_ref[1] + first + 8 * t + row_idx
                ok = x_ok & (y_idx >= 0) & (y_idx < extent_y)
                fresh = uc + damping * (rhs - image) / (total * half)
                o_ref[p, out_rows, :] = jnp.where(ok, fresh, 0.0)


def plane_step(offsets, u, b, k, scale, extent_x, extent_y, residual=False, inner=False):
    (u_arr, u_i), (b_arr, b_i), (k_arr, k_i) = u, b, k
    depth_x, depth_y, depth_z = u_arr.shape[-3:]
    chunk = 4 if inner else CHUNK
    lead_blocks = 1 if inner else 0
    chunks = (depth_x - 8 * lead_blocks) // chunk

    def spec(arr, idx, kind):
        lead = (None,) if arr.ndim == 4 else ()
        pre = (idx,) if arr.ndim == 4 else ()
        if kind == "main":
            return pl.BlockSpec(lead + (chunk, depth_y, depth_z),
                                lambda i, off: pre + (i + lead_blocks, 0, 0))
        if kind == "lo":
            return pl.BlockSpec(lead + (1, depth_y, depth_z),
                                lambda i, off: pre + (jnp.maximum((i + lead_blocks) * chunk - 1, 0), 0, 0))
        return pl.BlockSpec(lead + (1, depth_y, depth_z),
                            lambda i, off: pre + (jnp.minimum((i + lead_blocks) * chunk + chunk, depth_x - 1), 0, 0))

    kernel = functools.partial(_plane_kernel, scale=scale, extent_x=extent_x, extent_y=extent_y,
                               residual=residual, chunk=chunk, inner=inner)
    out_x = depth_x - 8 if inner else depth_x
    out_y = depth_y - 8 if inner else depth_y
    grid_spec = pltpu.PrefetchScalarGridSpec(
        num_scalar_prefetch=1,
        grid=(chunks,),
        in_specs=[spec(u_arr, u_i, "main"), spec(u_arr, u_i, "lo"), spec(u_arr, u_i, "hi"),
                  spec(b_arr, b_i, "main"),
                  spec(k_arr, k_i, "main"), spec(k_arr, k_i, "lo"), spec(k_arr, k_i, "hi")],
        out_specs=pl.BlockSpec((chunk, out_y, depth_z), lambda i, off: (i, 0, 0)),
    )
    cells = out_x * out_y * depth_z
    return pl.pallas_call(
        kernel,
        grid_spec=grid_spec,
        out_shape=jax.ShapeDtypeStruct((out_x, out_y, depth_z), jnp.float32),
        compiler_params=pltpu.CompilerParams(dimension_semantics=("arbitrary",)),
        cost_estimate=pl.CostEstimate(flops=45 * cells, transcendentals=0, bytes_accessed=4 * 4 * cells),
    )(offsets, u_arr, u_arr, u_arr, b_arr, k_arr, k_arr, k_arr)


def _sweep_planes(off_ref, u_ref, b_ref, k_ref, o_ref, *, scale, extent_x, extent_y, residual,
                  planes, inner):
    depth_y, depth_z = u_ref.shape[-2], u_ref.shape[-1]
    first = 4 if inner else 0
    tiles = (depth_y - 2 * first) // 8
    half = 0.5 * scale
    z_idx = lax.broadcasted_iota(jnp.int32, (8, depth_z), 1)
    z_first = z_idx == 0
    z_last = z_idx == depth_z - 1
    row_idx = lax.broadcasted_iota(jnp.int32, (8, depth_z), 0)

    def z_lo(a):
        return jnp.where(z_first, 0.0, pltpu.roll(a, 1, 1))

    def z_hi(a):
        return jnp.where(z_last, 0.0, pltpu.roll(a, depth_z - 1, 1))

    def rows(ref, plane, t, shift):
        start = first + 8 * t
        if shift == 0:
            return ref[plane, pl.ds(start, 8), :]
        if shift < 0 and start == 0:
            return pltpu.roll(ref[plane, pl.ds(0, 8), :], 1, 0)
        if shift > 0 and start + 8 == depth_y:
            return pltpu.roll(ref[plane, pl.ds(start, 8), :], 7, 0)
        return ref[plane, pl.ds(start + shift, 8), :]

    def plane_body(p, carry):
        x_idx = off_ref[0] + p
        x_ok = (x_idx >= 0) & (x_idx < extent_x)
        out_plane = p - first
        for t in range(tiles):
            kc = rows(k_ref, p, t, 0)
            uc = rows(u_ref, p, t, 0)
            sxm = kc + rows(k_ref, p - 1, t, 0)
            sxp = rows(k_ref, p + 1, t, 0) + kc
            sym = kc + rows(k_ref, p, t, -1)
            syp = rows(k_ref, p, t, 1) + kc
            szm = kc + z_lo(kc)
            szp = z_hi(kc) + kc
            total = sxm + sxp + sym + syp + szm + szp
            beside = sxm * rows(u_ref, p - 1, t, 0) + sxp * rows(u_ref, p + 1, t, 0)
            beside = beside + sym * rows(u_ref, p, t, -1) + syp * rows(u_ref, p, t, 1)
            beside = beside + szm * z_lo(uc) + szp * z_hi(uc)
            image = (total * uc - beside) * half
            rhs = rows(b_ref, p, t, 0)
            out_rows = pl.ds(8 * t if inner else first + 8 * t, 8)
            if residual:
                o_ref[out_plane, out_rows, :] = rhs - image
            else:
                y_idx = off_ref[1] + first + 8 * t + row_idx
                ok = x_ok & (y_idx >= 0) & (y_idx < extent_y)
                fresh = uc + damping * (rhs - image) / (total * half)
                o_ref[out_plane, out_rows, :] = jnp.where(ok, fresh, 0.0)
        return carry

    lax.fori_loop(planes[0], planes[1], plane_body, 0)


def _down_kernel(off_ref, s_ref, u2_ref, r_ref, u1_ref, *, extent_x, extent_y):
    depth_x = s_ref.shape[1]
    common = dict(scale=1.0, extent_x=extent_x, extent_y=extent_y)
    _sweep_planes(off_ref, s_ref.at[0], s_ref.at[1], s_ref.at[2], u1_ref, residual=False,
                  planes=(1, depth_x - 1), inner=False, **common)
    _sweep_planes(off_ref, u1_ref, s_ref.at[1], s_ref.at[2], u2_ref, residual=False,
                  planes=(2, depth_x - 2), inner=False, **common)
    _sweep_planes(off_ref, u2_ref, s_ref.at[1], s_ref.at[2], r_ref, residual=True,
                  planes=(4, depth_x - 4), inner=True, **common)


def _up_kernel(off_ref, u3_ref, s_ref, u5_ref, u4_ref, *, extent_x, extent_y):
    depth_x = s_ref.shape[1]
    common = dict(scale=1.0, extent_x=extent_x, extent_y=extent_y)
    _sweep_planes(off_ref, u3_ref, s_ref.at[1], s_ref.at[2], u4_ref, residual=False,
                  planes=(3, depth_x - 3), inner=False, **common)
    _sweep_planes(off_ref, u4_ref, s_ref.at[1], s_ref.at[2], u5_ref, residual=False,
                  planes=(4, depth_x - 4), inner=True, **common)


def _frame_call(kernel, offsets, arrays, outs, scratch, cells, passes):
    vmem = pl.BlockSpec(memory_space=pltpu.VMEM)
    return pl.pallas_call(
        kernel,
        grid=(1,),
        out_shape=outs,
        in_specs=[pl.BlockSpec(memory_space=pltpu.SMEM)] + [vmem] * len(arrays),
        out_specs=[vmem] * len(outs) if isinstance(outs, (list, tuple)) else vmem,
        scratch_shapes=scratch,
        compiler_params=pltpu.CompilerParams(vmem_limit_bytes=60 * 1024 * 1024),
        cost_estimate=pl.CostEstimate(flops=40 * cells * passes, transcendentals=0,
                                      bytes_accessed=4 * 5 * cells),
    )(offsets, *arrays)


def on_device(start_field, source, conductance):
    nx, ny = start_field.shape[0], start_field.shape[1]
    mx, my = nx // 2, ny // 2
    lx, ly = nx // 4, ny // 4

    with jax.named_scope("level0_down"):
        fine = exchange(jnp.stack([start_field, source, conductance]), 4)
        extent_x, extent_y = nx * lax.axis_size("row"), ny * lax.axis_size("col")
        offsets = jnp.stack([lax.axis_index("row") * nx - 4, lax.axis_index("col") * ny - 4]).astype(jnp.int32)
        depth_x, depth_y, depth_z = fine.shape[1:]
        frame = jax.ShapeDtypeStruct((depth_x, depth_y, depth_z), jnp.float32)
        inner = jax.ShapeDtypeStruct((depth_x - 8, depth_y - 8, depth_z), jnp.float32)
        kernel = functools.partial(_down_kernel, extent_x=extent_x, extent_y=extent_y)
        u2, residual = _frame_call(kernel, offsets, [fine], [frame, inner],
                                   [pltpu.VMEM(frame.shape, jnp.float32)], fine[0].size, 3)
        mid_rhs = restrict_mean(residual)
        mid_cond = restrict_mean(conductance)

    with jax.named_scope("level1_down"):
        mid = exchange(jnp.stack([mid_rhs, mid_cond]), 4)
        rhs1, k1 = mid[0], mid[1]
        e1 = first_guess(trim(rhs1, 1), k1, 0.25, grid_mask(mx, my, 3))
        e1 = sweep(e1, trim(rhs1, 2), trim(k1, 1), 0.25, grid_mask(mx, my, 2))
        image = operate(trim(e1, 1), trim(k1, 3), 0.25)[0]
        low_rhs = restrict_mean(mid_rhs - image)
        low_cond = restrict_mean(mid_cond)

    with jax.named_scope("level2"):
        low = exchange(jnp.stack([low_rhs, low_cond]), 5)
        rhs2, k2 = low[0], low[1]
        e2 = first_guess(trim(rhs2, 1), k2, 0.0625, grid_mask(lx, ly, 4))
        for halo in (3, 2, 1):
            e2 = sweep(e2, trim(rhs2, 5 - halo), trim(k2, 4 - halo), 0.0625, grid_mask(lx, ly, halo))

    with jax.named_scope("level1_up"):
        e1 = e1 + prolong_copy(e2)
        e1 = sweep(e1, trim(rhs1, 3), trim(k1, 2), 0.25, grid_mask(mx, my, 1))

    with jax.named_scope("level0_up"):
        u3 = u2 + jnp.pad(prolong_copy(e1), ((2, 2), (2, 2), (0, 0)))
        kernel = functools.partial(_up_kernel, extent_x=extent_x, extent_y=extent_y)
        u5 = _frame_call(kernel, offsets, [u3, fine], inner, [pltpu.VMEM(frame.shape, jnp.float32)],
                         fine[0].size, 2)
    return u5


def solution(mesh):
    placed = (P("row", "col", None), P("row", "col", None), P("row", "col", None))
    return jax.shard_map(
        on_device, mesh=mesh, in_specs=placed, out_specs=P("row", "col", None), check_vma=False
    )
```

```python
import functools

import jax
import jax.numpy as jnp
from jax import lax
from jax.experimental import pallas as pl
from jax.experimental.pallas import tpu as pltpu
from jax.sharding import PartitionSpec as P

damping = 2.0 / 3.0


def exchange(stack, width):
    for axis, dim in (("row", 1), ("col", 2)):
        count = lax.axis_size(axis)
        forward = [(i, i + 1) for i in range(count - 1)]
        backward = [(i + 1, i) for i in range(count - 1)]
        size = stack.shape[dim]
        low = lax.ppermute(lax.slice_in_dim(stack, size - width, size, axis=dim), axis, forward)
        high = lax.ppermute(lax.slice_in_dim(stack, 0, width, axis=dim), axis, backward)
        stack = jnp.concatenate([low, stack, high], axis=dim)
    return stack


def trim(field, k):
    if k == 0:
        return field
    return field[k:-k, k:-k]


def grid_mask(nx, ny, halo):
    rows = lax.axis_size("row")
    cols = lax.axis_size("col")
    gx = lax.axis_index("row") * nx - halo + lax.broadcasted_iota(jnp.int32, (nx + 2 * halo, 1, 1), 0)
    gy = lax.axis_index("col") * ny - halo + lax.broadcasted_iota(jnp.int32, (1, ny + 2 * halo, 1), 1)
    return ((gx >= 0) & (gx < nx * rows)) & ((gy >= 0) & (gy < ny * cols))


def z_lo(field):
    depth_idx = lax.broadcasted_iota(jnp.int32, field.shape, field.ndim - 1)
    return jnp.where(depth_idx == 0, 0.0, jnp.roll(field, 1, field.ndim - 1))


def z_hi(field):
    depth_idx = lax.broadcasted_iota(jnp.int32, field.shape, field.ndim - 1)
    return jnp.where(depth_idx == field.shape[-1] - 1, 0.0, jnp.roll(field, -1, field.ndim - 1))


def coefs(cond, scale):
    half = 0.5 * scale
    centre = cond[1:-1, 1:-1]
    wxm = (centre + cond[:-2, 1:-1]) * half
    wxp = (cond[2:, 1:-1] + centre) * half
    wym = (centre + cond[1:-1, :-2]) * half
    wyp = (cond[1:-1, 2:] + centre) * half
    wzm = (centre + z_lo(centre)) * half
    wzp = (z_hi(centre) + centre) * half
    diagonal = wxm + wxp + wym + wyp + wzm + wzp
    return wxm, wxp, wym, wyp, wzm, wzp, diagonal


def operate(field, cond, scale):
    wxm, wxp, wym, wyp, wzm, wzp, diagonal = coefs(cond, scale)
    centre = field[1:-1, 1:-1]
    beside = wxm * field[:-2, 1:-1] + wxp * field[2:, 1:-1]
    beside = beside + wym * field[1:-1, :-2] + wyp * field[1:-1, 2:]
    beside = beside + wzm * z_lo(centre) + wzp * z_hi(centre)
    return diagonal * centre - beside, diagonal, centre


def sweep(field, rhs, cond, scale, mask):
    image, diagonal, centre = operate(field, cond, scale)
    return jnp.where(mask, centre + damping * (rhs - image) / diagonal, 0.0)


def first_guess(rhs, cond, scale, mask):
    diagonal = coefs(cond, scale)[6]
    return jnp.where(mask, damping * rhs / diagonal, 0.0)


def restrict_mean(field):
    depth = field.shape[2]
    planar = field.reshape(field.shape[0] // 2, 2, field.shape[1] // 2, 2, depth).sum(axis=(1, 3))
    fine_idx = lax.broadcasted_iota(jnp.int32, (depth, depth // 2), 0)
    coarse_idx = lax.broadcasted_iota(jnp.int32, (depth, depth // 2), 1)
    table = jnp.where(fine_idx // 2 == coarse_idx, 0.125, 0.0).astype(jnp.float32)
    return jnp.dot(
        planar, table, precision=lax.Precision.HIGHEST, preferred_element_type=jnp.float32
    )


def prolong_copy(field):
    depth = field.shape[2]
    coarse_idx = lax.broadcasted_iota(jnp.int32, (depth, 2 * depth), 0)
    fine_idx = lax.broadcasted_iota(jnp.int32, (depth, 2 * depth), 1)
    table = jnp.where(fine_idx // 2 == coarse_idx, 1.0, 0.0).astype(jnp.float32)
    deeper = jnp.dot(
        field, table, precision=lax.Precision.HIGHEST, preferred_element_type=jnp.float32
    )
    return jnp.repeat(jnp.repeat(deeper, 2, 0), 2, 1)


CHUNK = 8


def _plane_kernel(off_ref, u_ref, ulo_ref, uhi_ref, b_ref, k_ref, klo_ref, khi_ref, o_ref, *,
                  scale, extent_x, extent_y, residual, chunk, inner):
    step = pl.program_id(0)
    depth_y, depth_z = u_ref.shape[-2], u_ref.shape[-1]
    first = 4 if inner else 0
    tiles = (depth_y - 2 * first) // 8
    half = 0.5 * scale
    z_idx = lax.broadcasted_iota(jnp.int32, (8, depth_z), 1)
    z_first = z_idx == 0
    z_last = z_idx == depth_z - 1
    row_idx = lax.broadcasted_iota(jnp.int32, (8, depth_z), 0)

    def z_lo(a):
        return jnp.where(z_first, 0.0, pltpu.roll(a, 1, 1))

    def z_hi(a):
        return jnp.where(z_last, 0.0, pltpu.roll(a, depth_z - 1, 1))

    def rows(ref, plane, t, shift):
        start = first + 8 * t
        if shift == 0:
            return ref[plane, pl.ds(start, 8), :]
        if shift < 0 and start == 0:
            return pltpu.roll(ref[plane, pl.ds(0, 8), :], 1, 0)
        if shift > 0 and start + 8 == depth_y:
            return pltpu.roll(ref[plane, pl.ds(start, 8), :], 7, 0)
        return ref[plane, pl.ds(start + shift, 8), :]

    for p in range(chunk):
        k_m = (klo_ref, 0) if p == 0 else (k_ref, p - 1)
        k_p = (khi_ref, 0) if p == chunk - 1 else (k_ref, p + 1)
        u_m = (ulo_ref, 0) if p == 0 else (u_ref, p - 1)
        u_p = (uhi_ref, 0) if p == chunk - 1 else (u_ref, p + 1)
        x_idx = off_ref[0] + first + step * chunk + p
        x_ok = (x_idx >= 0) & (x_idx < extent_x)
        for t in range(tiles):
            kc = rows(k_ref, p, t, 0)
            uc = rows(u_ref, p, t, 0)
            sxm = kc + rows(k_m[0], k_m[1], t, 0)
            sxp = rows(k_p[0], k_p[1], t, 0) + kc
            sym = kc + rows(k_ref, p, t, -1)
            syp = rows(k_ref, p, t, 1) + kc
            szm = kc + z_lo(kc)
            szp = z_hi(kc) + kc
            total = sxm + sxp + sym + syp + szm + szp
            beside = sxm * rows(u_m[0], u_m[1], t, 0) + sxp * rows(u_p[0], u_p[1], t, 0)
            beside = beside + sym * rows(u_ref, p, t, -1) + syp * rows(u_ref, p, t, 1)
            beside = beside + szm * z_lo(uc) + szp * z_hi(uc)
            image = (total * uc - beside) * half
            rhs = rows(b_ref, p, t, 0)
            out_rows = pl.ds(8 * t if inner else first + 8 * t, 8)
            if residual:
                o_ref[p, out_rows, :] = rhs - image
            else:
                y_idx = off_ref[1] + first + 8 * t + row_idx
                ok = x_ok & (y_idx >= 0) & (y_idx < extent_y)
                fresh = uc + damping * (rhs - image) / (total * half)
                o_ref[p, out_rows, :] = jnp.where(ok, fresh, 0.0)


def plane_step(offsets, u, b, k, scale, extent_x, extent_y, residual=False, inner=False):
    (u_arr, u_i), (b_arr, b_i), (k_arr, k_i) = u, b, k
    depth_x, depth_y, depth_z = u_arr.shape[-3:]
    chunk = 4 if inner else CHUNK
    lead_blocks = 1 if inner else 0
    chunks = (depth_x - 8 * lead_blocks) // chunk

    def spec(arr, idx, kind):
        lead = (None,) if arr.ndim == 4 else ()
        pre = (idx,) if arr.ndim == 4 else ()
        if kind == "main":
            return pl.BlockSpec(lead + (chunk, depth_y, depth_z),
                                lambda i, off: pre + (i + lead_blocks, 0, 0))
        if kind == "lo":
            return pl.BlockSpec(lead + (1, depth_y, depth_z),
                                lambda i, off: pre + (jnp.maximum((i + lead_blocks) * chunk - 1, 0), 0, 0))
        return pl.BlockSpec(lead + (1, depth_y, depth_z),
                            lambda i, off: pre + (jnp.minimum((i + lead_blocks) * chunk + chunk, depth_x - 1), 0, 0))

    kernel = functools.partial(_plane_kernel, scale=scale, extent_x=extent_x, extent_y=extent_y,
                               residual=residual, chunk=chunk, inner=inner)
    out_x = depth_x - 8 if inner else depth_x
    out_y = depth_y - 8 if inner else depth_y
    grid_spec = pltpu.PrefetchScalarGridSpec(
        num_scalar_prefetch=1,
        grid=(chunks,),
        in_specs=[spec(u_arr, u_i, "main"), spec(u_arr, u_i, "lo"), spec(u_arr, u_i, "hi"),
                  spec(b_arr, b_i, "main"),
                  spec(k_arr, k_i, "main"), spec(k_arr, k_i, "lo"), spec(k_arr, k_i, "hi")],
        out_specs=pl.BlockSpec((chunk, out_y, depth_z), lambda i, off: (i, 0, 0)),
    )
    cells = out_x * out_y * depth_z
    return pl.pallas_call(
        kernel,
        grid_spec=grid_spec,
        out_shape=jax.ShapeDtypeStruct((out_x, out_y, depth_z), jnp.float32),
        compiler_params=pltpu.CompilerParams(dimension_semantics=("arbitrary",)),
        cost_estimate=pl.CostEstimate(flops=45 * cells, transcendentals=0, bytes_accessed=4 * 4 * cells),
    )(offsets, u_arr, u_arr, u_arr, b_arr, k_arr, k_arr, k_arr)


def _sweep_planes(off_ref, u_ref, b_ref, k_ref, o_ref, *, scale, extent_x, extent_y, residual,
                  planes, inner):
    depth_y, depth_z = u_ref.shape[-2], u_ref.shape[-1]
    first = 4 if inner else 0
    tiles = (depth_y - 2 * first) // 8
    half = 0.5 * scale
    z_idx = lax.broadcasted_iota(jnp.int32, (8, depth_z), 1)
    z_first = z_idx == 0
    z_last = z_idx == depth_z - 1
    row_idx = lax.broadcasted_iota(jnp.int32, (8, depth_z), 0)

    def z_lo(a):
        return jnp.where(z_first, 0.0, pltpu.roll(a, 1, 1))

    def z_hi(a):
        return jnp.where(z_last, 0.0, pltpu.roll(a, depth_z - 1, 1))

    def rows(ref, plane, t, shift):
        start = first + 8 * t
        if shift == 0:
            return ref[plane, pl.ds(start, 8), :]
        if shift < 0 and start == 0:
            return pltpu.roll(ref[plane, pl.ds(0, 8), :], 1, 0)
        if shift > 0 and start + 8 == depth_y:
            return pltpu.roll(ref[plane, pl.ds(start, 8), :], 7, 0)
        return ref[plane, pl.ds(start + shift, 8), :]

    def plane_body(p, carry):
        x_idx = off_ref[0] + p
        x_ok = (x_idx >= 0) & (x_idx < extent_x)
        out_plane = p - first
        for t in range(tiles):
            kc = rows(k_ref, p, t, 0)
            uc = rows(u_ref, p, t, 0)
            sxm = kc + rows(k_ref, p - 1, t, 0)
            sxp = rows(k_ref, p + 1, t, 0) + kc
            sym = kc + rows(k_ref, p, t, -1)
            syp = rows(k_ref, p, t, 1) + kc
            szm = kc + z_lo(kc)
            szp = z_hi(kc) + kc
            total = sxm + sxp + sym + syp + szm + szp
            beside = sxm * rows(u_ref, p - 1, t, 0) + sxp * rows(u_ref, p + 1, t, 0)
            beside = beside + sym * rows(u_ref, p, t, -1) + syp * rows(u_ref, p, t, 1)
            beside = beside + szm * z_lo(uc) + szp * z_hi(uc)
            image = (total * uc - beside) * half
            rhs = rows(b_ref, p, t, 0)
            out_rows = pl.ds(8 * t if inner else first + 8 * t, 8)
            if residual:
                o_ref[out_plane, out_rows, :] = rhs - image
            else:
                y_idx = off_ref[1] + first + 8 * t + row_idx
                ok = x_ok & (y_idx >= 0) & (y_idx < extent_y)
                fresh = uc + damping * (rhs - image) / (total * half)
                o_ref[out_plane, out_rows, :] = jnp.where(ok, fresh, 0.0)
        return carry

    lax.fori_loop(planes[0], planes[1], plane_body, 0)


def _down_kernel(off_ref, s_ref, u2_ref, r_ref, u1_ref, *, extent_x, extent_y):
    depth_x = s_ref.shape[1]
    common = dict(scale=1.0, extent_x=extent_x, extent_y=extent_y)
    _sweep_planes(off_ref, s_ref.at[0], s_ref.at[1], s_ref.at[2], u1_ref, residual=False,
                  planes=(1, depth_x - 1), inner=False, **common)
    _sweep_planes(off_ref, u1_ref, s_ref.at[1], s_ref.at[2], u2_ref, residual=False,
                  planes=(2, depth_x - 2), inner=False, **common)
    _sweep_planes(off_ref, u2_ref, s_ref.at[1], s_ref.at[2], r_ref, residual=True,
                  planes=(4, depth_x - 4), inner=True, **common)


def _up_kernel(off_ref, u2_ref, e_ref, s_ref, u5_ref, u3_ref, u4_ref, *, extent_x, extent_y):
    depth_x = s_ref.shape[1]
    common = dict(scale=1.0, extent_x=extent_x, extent_y=extent_y)

    def add_plane(p, carry):
        u3_ref[p] = u2_ref[p] + e_ref[p // 2 - 1]
        return carry

    lax.fori_loop(2, depth_x - 2, add_plane, 0)
    _sweep_planes(off_ref, u3_ref, s_ref.at[1], s_ref.at[2], u4_ref, residual=False,
                  planes=(3, depth_x - 3), inner=False, **common)
    _sweep_planes(off_ref, u4_ref, s_ref.at[1], s_ref.at[2], u5_ref, residual=False,
                  planes=(4, depth_x - 4), inner=True, **common)


def _frame_call(kernel, offsets, arrays, outs, scratch, cells, passes):
    vmem = pl.BlockSpec(memory_space=pltpu.VMEM)
    return pl.pallas_call(
        kernel,
        grid=(1,),
        out_shape=outs,
        in_specs=[pl.BlockSpec(memory_space=pltpu.SMEM)] + [vmem] * len(arrays),
        out_specs=[vmem] * len(outs) if isinstance(outs, (list, tuple)) else vmem,
        scratch_shapes=scratch,
        compiler_params=pltpu.CompilerParams(vmem_limit_bytes=60 * 1024 * 1024),
        cost_estimate=pl.CostEstimate(flops=40 * cells * passes, transcendentals=0,
                                      bytes_accessed=4 * 5 * cells),
    )(offsets, *arrays)


def on_device(start_field, source, conductance):
    nx, ny = start_field.shape[0], start_field.shape[1]
    mx, my = nx // 2, ny // 2
    lx, ly = nx // 4, ny // 4

    with jax.named_scope("level0_down"):
        fine = exchange(jnp.stack([start_field, source, conductance]), 4)
        extent_x, extent_y = nx * lax.axis_size("row"), ny * lax.axis_size("col")
        offsets = jnp.stack([lax.axis_index("row") * nx - 4, lax.axis_index("col") * ny - 4]).astype(jnp.int32)
        depth_x, depth_y, depth_z = fine.shape[1:]
        frame = jax.ShapeDtypeStruct((depth_x, depth_y, depth_z), jnp.float32)
        inner = jax.ShapeDtypeStruct((depth_x - 8, depth_y - 8, depth_z), jnp.float32)
        kernel = functools.partial(_down_kernel, extent_x=extent_x, extent_y=extent_y)
        u2, residual = _frame_call(kernel, offsets, [fine], [frame, inner],
                                   [pltpu.VMEM(frame.shape, jnp.float32)], fine[0].size, 3)
        mid_rhs = restrict_mean(residual)
        mid_cond = restrict_mean(conductance)

    with jax.named_scope("level1_down"):
        mid = exchange(jnp.stack([mid_rhs, mid_cond]), 4)
        rhs1, k1 = mid[0], mid[1]
        e1 = first_guess(trim(rhs1, 1), k1, 0.25, grid_mask(mx, my, 3))
        e1 = sweep(e1, trim(rhs1, 2), trim(k1, 1), 0.25, grid_mask(mx, my, 2))
        image = operate(trim(e1, 1), trim(k1, 3), 0.25)[0]
        low_rhs = restrict_mean(mid_rhs - image)
        low_cond = restrict_mean(mid_cond)

    with jax.named_scope("level2"):
        low = exchange(jnp.stack([low_rhs, low_cond]), 5)
        rhs2, k2 = low[0], low[1]
        e2 = first_guess(trim(rhs2, 1), k2, 0.0625, grid_mask(lx, ly, 4))
        for halo in (3, 2, 1):
            e2 = sweep(e2, trim(rhs2, 5 - halo), trim(k2, 4 - halo), 0.0625, grid_mask(lx, ly, halo))

    with jax.named_scope("level1_up"):
        e1 = e1 + prolong_copy(e2)
        e1 = sweep(e1, trim(rhs1, 3), trim(k1, 2), 0.25, grid_mask(mx, my, 1))

    with jax.named_scope("level0_up"):
        coarse_z = e1.shape[2]
        coarse_idx = lax.broadcasted_iota(jnp.int32, (coarse_z, 2 * coarse_z), 0)
        fine_idx = lax.broadcasted_iota(jnp.int32, (coarse_z, 2 * coarse_z), 1)
        table = jnp.where(fine_idx // 2 == coarse_idx, 1.0, 0.0).astype(jnp.float32)
        deeper = jnp.dot(e1, table, precision=lax.Precision.HIGHEST, preferred_element_type=jnp.float32)
        wider = jnp.pad(jnp.repeat(deeper, 2, 1), ((0, 0), (2, 2), (0, 0)))
        kernel = functools.partial(_up_kernel, extent_x=extent_x, extent_y=extent_y)
        u5 = _frame_call(kernel, offsets, [u2, wider, fine], inner,
                         [pltpu.VMEM(frame.shape, jnp.float32), pltpu.VMEM(frame.shape, jnp.float32)],
                         fine[0].size, 2)
    return u5


def solution(mesh):
    placed = (P("row", "col", None), P("row", "col", None), P("row", "col", None))
    return jax.shard_map(
        on_device, mesh=mesh, in_specs=placed, out_specs=P("row", "col", None), check_vma=False
    )
```

```python
import functools

import jax
import jax.numpy as jnp
from jax import lax
from jax.experimental import pallas as pl
from jax.experimental.pallas import tpu as pltpu
from jax.sharding import PartitionSpec as P

damping = 2.0 / 3.0


def exchange(stack, width):
    for axis, dim in (("col", 2), ("row", 1)):
        count = lax.axis_size(axis)
        forward = [(i, i + 1) for i in range(count - 1)]
        backward = [(i + 1, i) for i in range(count - 1)]
        size = stack.shape[dim]
        low = lax.ppermute(lax.slice_in_dim(stack, size - width, size, axis=dim), axis, forward)
        high = lax.ppermute(lax.slice_in_dim(stack, 0, width, axis=dim), axis, backward)
        stack = jnp.concatenate([low, stack, high], axis=dim)
    return stack


def trim(field, k):
    if k == 0:
        return field
    return field[k:-k, k:-k]


def grid_mask(nx, ny, halo):
    rows = lax.axis_size("row")
    cols = lax.axis_size("col")
    gx = lax.axis_index("row") * nx - halo + lax.broadcasted_iota(jnp.int32, (nx + 2 * halo, 1, 1), 0)
    gy = lax.axis_index("col") * ny - halo + lax.broadcasted_iota(jnp.int32, (1, ny + 2 * halo, 1), 1)
    return ((gx >= 0) & (gx < nx * rows)) & ((gy >= 0) & (gy < ny * cols))


def z_lo(field):
    depth_idx = lax.broadcasted_iota(jnp.int32, field.shape, field.ndim - 1)
    return jnp.where(depth_idx == 0, 0.0, jnp.roll(field, 1, field.ndim - 1))


def z_hi(field):
    depth_idx = lax.broadcasted_iota(jnp.int32, field.shape, field.ndim - 1)
    return jnp.where(depth_idx == field.shape[-1] - 1, 0.0, jnp.roll(field, -1, field.ndim - 1))


def coefs(cond, scale):
    half = 0.5 * scale
    centre = cond[1:-1, 1:-1]
    wxm = (centre + cond[:-2, 1:-1]) * half
    wxp = (cond[2:, 1:-1] + centre) * half
    wym = (centre + cond[1:-1, :-2]) * half
    wyp = (cond[1:-1, 2:] + centre) * half
    wzm = (centre + z_lo(centre)) * half
    wzp = (z_hi(centre) + centre) * half
    diagonal = wxm + wxp + wym + wyp + wzm + wzp
    return wxm, wxp, wym, wyp, wzm, wzp, diagonal


def operate(field, cond, scale):
    wxm, wxp, wym, wyp, wzm, wzp, diagonal = coefs(cond, scale)
    centre = field[1:-1, 1:-1]
    beside = wxm * field[:-2, 1:-1] + wxp * field[2:, 1:-1]
    beside = beside + wym * field[1:-1, :-2] + wyp * field[1:-1, 2:]
    beside = beside + wzm * z_lo(centre) + wzp * z_hi(centre)
    return diagonal * centre - beside, diagonal, centre


def sweep(field, rhs, cond, scale, mask):
    image, diagonal, centre = operate(field, cond, scale)
    return jnp.where(mask, centre + damping * (rhs - image) / diagonal, 0.0)


def first_guess(rhs, cond, scale, mask):
    diagonal = coefs(cond, scale)[6]
    return jnp.where(mask, damping * rhs / diagonal, 0.0)


def restrict_mean(field):
    depth = field.shape[2]
    planar = field.reshape(field.shape[0] // 2, 2, field.shape[1] // 2, 2, depth).sum(axis=(1, 3))
    fine_idx = lax.broadcasted_iota(jnp.int32, (depth, depth // 2), 0)
    coarse_idx = lax.broadcasted_iota(jnp.int32, (depth, depth // 2), 1)
    table = jnp.where(fine_idx // 2 == coarse_idx, 0.125, 0.0).astype(jnp.float32)
    return jnp.dot(
        planar, table, precision=lax.Precision.HIGHEST, preferred_element_type=jnp.float32
    )


def prolong_copy(field):
    depth = field.shape[2]
    coarse_idx = lax.broadcasted_iota(jnp.int32, (depth, 2 * depth), 0)
    fine_idx = lax.broadcasted_iota(jnp.int32, (depth, 2 * depth), 1)
    table = jnp.where(fine_idx // 2 == coarse_idx, 1.0, 0.0).astype(jnp.float32)
    deeper = jnp.dot(
        field, table, precision=lax.Precision.HIGHEST, preferred_element_type=jnp.float32
    )
    return jnp.repeat(jnp.repeat(deeper, 2, 0), 2, 1)


CHUNK = 8


def _plane_kernel(off_ref, u_ref, ulo_ref, uhi_ref, b_ref, k_ref, klo_ref, khi_ref, o_ref, *,
                  scale, extent_x, extent_y, residual, chunk, inner):
    step = pl.program_id(0)
    depth_y, depth_z = u_ref.shape[-2], u_ref.shape[-1]
    first = 4 if inner else 0
    tiles = (depth_y - 2 * first) // 8
    half = 0.5 * scale
    z_idx = lax.broadcasted_iota(jnp.int32, (8, depth_z), 1)
    z_first = z_idx == 0
    z_last = z_idx == depth_z - 1
    row_idx = lax.broadcasted_iota(jnp.int32, (8, depth_z), 0)

    def z_lo(a):
        return jnp.where(z_first, 0.0, pltpu.roll(a, 1, 1))

    def z_hi(a):
        return jnp.where(z_last, 0.0, pltpu.roll(a, depth_z - 1, 1))

    def rows(ref, plane, t, shift):
        start = first + 8 * t
        if shift == 0:
            return ref[plane, pl.ds(start, 8), :]
        if shift < 0 and start == 0:
            return pltpu.roll(ref[plane, pl.ds(0, 8), :], 1, 0)
        if shift > 0 and start + 8 == depth_y:
            return pltpu.roll(ref[plane, pl.ds(start, 8), :], 7, 0)
        return ref[plane, pl.ds(start + shift, 8), :]

    for p in range(chunk):
        k_m = (klo_ref, 0) if p == 0 else (k_ref, p - 1)
        k_p = (khi_ref, 0) if p == chunk - 1 else (k_ref, p + 1)
        u_m = (ulo_ref, 0) if p == 0 else (u_ref, p - 1)
        u_p = (uhi_ref, 0) if p == chunk - 1 else (u_ref, p + 1)
        x_idx = off_ref[0] + first + step * chunk + p
        x_ok = (x_idx >= 0) & (x_idx < extent_x)
        for t in range(tiles):
            kc = rows(k_ref, p, t, 0)
            uc = rows(u_ref, p, t, 0)
            sxm = kc + rows(k_m[0], k_m[1], t, 0)
            sxp = rows(k_p[0], k_p[1], t, 0) + kc
            sym = kc + rows(k_ref, p, t, -1)
            syp = rows(k_ref, p, t, 1) + kc
            szm = kc + z_lo(kc)
            szp = z_hi(kc) + kc
            total = sxm + sxp + sym + syp + szm + szp
            beside = sxm * rows(u_m[0], u_m[1], t, 0) + sxp * rows(u_p[0], u_p[1], t, 0)
            beside = beside + sym * rows(u_ref, p, t, -1) + syp * rows(u_ref, p, t, 1)
            beside = beside + szm * z_lo(uc) + szp * z_hi(uc)
            image = (total * uc - beside) * half
            rhs = rows(b_ref, p, t, 0)
            out_rows = pl.ds(8 * t if inner else first + 8 * t, 8)
            if residual:
                o_ref[p, out_rows, :] = rhs - image
            else:
                y_idx = off_ref[1] + first + 8 * t + row_idx
                ok = x_ok & (y_idx >= 0) & (y_idx < extent_y)
                fresh = uc + damping * (rhs - image) / (total * half)
                o_ref[p, out_rows, :] = jnp.where(ok, fresh, 0.0)


def plane_step(offsets, u, b, k, scale, extent_x, extent_y, residual=False, inner=False):
    (u_arr, u_i), (b_arr, b_i), (k_arr, k_i) = u, b, k
    depth_x, depth_y, depth_z = u_arr.shape[-3:]
    chunk = 4 if inner else CHUNK
    lead_blocks = 1 if inner else 0
    chunks = (depth_x - 8 * lead_blocks) // chunk

    def spec(arr, idx, kind):
        lead = (None,) if arr.ndim == 4 else ()
        pre = (idx,) if arr.ndim == 4 else ()
        if kind == "main":
            return pl.BlockSpec(lead + (chunk, depth_y, depth_z),
                                lambda i, off: pre + (i + lead_blocks, 0, 0))
        if kind == "lo":
            return pl.BlockSpec(lead + (1, depth_y, depth_z),
                                lambda i, off: pre + (jnp.maximum((i + lead_blocks) * chunk - 1, 0), 0, 0))
        return pl.BlockSpec(lead + (1, depth_y, depth_z),
                            lambda i, off: pre + (jnp.minimum((i + lead_blocks) * chunk + chunk, depth_x - 1), 0, 0))

    kernel = functools.partial(_plane_kernel, scale=scale, extent_x=extent_x, extent_y=extent_y,
                               residual=residual, chunk=chunk, inner=inner)
    out_x = depth_x - 8 if inner else depth_x
    out_y = depth_y - 8 if inner else depth_y
    grid_spec = pltpu.PrefetchScalarGridSpec(
        num_scalar_prefetch=1,
        grid=(chunks,),
        in_specs=[spec(u_arr, u_i, "main"), spec(u_arr, u_i, "lo"), spec(u_arr, u_i, "hi"),
                  spec(b_arr, b_i, "main"),
                  spec(k_arr, k_i, "main"), spec(k_arr, k_i, "lo"), spec(k_arr, k_i, "hi")],
        out_specs=pl.BlockSpec((chunk, out_y, depth_z), lambda i, off: (i, 0, 0)),
    )
    cells = out_x * out_y * depth_z
    return pl.pallas_call(
        kernel,
        grid_spec=grid_spec,
        out_shape=jax.ShapeDtypeStruct((out_x, out_y, depth_z), jnp.float32),
        compiler_params=pltpu.CompilerParams(dimension_semantics=("arbitrary",)),
        cost_estimate=pl.CostEstimate(flops=45 * cells, transcendentals=0, bytes_accessed=4 * 4 * cells),
    )(offsets, u_arr, u_arr, u_arr, b_arr, k_arr, k_arr, k_arr)


def _sweep_planes(off_ref, u_ref, b_ref, k_ref, o_ref, *, scale, extent_x, extent_y, residual,
                  planes, inner):
    depth_y, depth_z = u_ref.shape[-2], u_ref.shape[-1]
    first = 4 if inner else 0
    tiles = (depth_y - 2 * first) // 8
    half = 0.5 * scale
    z_idx = lax.broadcasted_iota(jnp.int32, (8, depth_z), 1)
    z_first = z_idx == 0
    z_last = z_idx == depth_z - 1
    row_idx = lax.broadcasted_iota(jnp.int32, (8, depth_z), 0)

    def z_lo(a):
        return jnp.where(z_first, 0.0, pltpu.roll(a, 1, 1))

    def z_hi(a):
        return jnp.where(z_last, 0.0, pltpu.roll(a, depth_z - 1, 1))

    def rows(ref, plane, t, shift):
        start = first + 8 * t
        if shift == 0:
            return ref[plane, pl.ds(start, 8), :]
        if shift < 0 and start == 0:
            return pltpu.roll(ref[plane, pl.ds(0, 8), :], 1, 0)
        if shift > 0 and start + 8 == depth_y:
            return pltpu.roll(ref[plane, pl.ds(start, 8), :], 7, 0)
        return ref[plane, pl.ds(start + shift, 8), :]

    def plane_body(p, carry):
        x_idx = off_ref[0] + p
        x_ok = (x_idx >= 0) & (x_idx < extent_x)
        out_plane = p - first
        for t in range(tiles):
            kc = rows(k_ref, p, t, 0)
            uc = rows(u_ref, p, t, 0)
            sxm = kc + rows(k_ref, p - 1, t, 0)
            sxp = rows(k_ref, p + 1, t, 0) + kc
            sym = kc + rows(k_ref, p, t, -1)
            syp = rows(k_ref, p, t, 1) + kc
            szm = kc + z_lo(kc)
            szp = z_hi(kc) + kc
            total = sxm + sxp + sym + syp + szm + szp
            beside = sxm * rows(u_ref, p - 1, t, 0) + sxp * rows(u_ref, p + 1, t, 0)
            beside = beside + sym * rows(u_ref, p, t, -1) + syp * rows(u_ref, p, t, 1)
            beside = beside + szm * z_lo(uc) + szp * z_hi(uc)
            image = (total * uc - beside) * half
            rhs = rows(b_ref, p, t, 0)
            out_rows = pl.ds(8 * t if inner else first + 8 * t, 8)
            if residual:
                o_ref[out_plane, out_rows, :] = rhs - image
            else:
                y_idx = off_ref[1] + first + 8 * t + row_idx
                ok = x_ok & (y_idx >= 0) & (y_idx < extent_y)
                fresh = uc + damping * (rhs - image) / (total * half)
                o_ref[out_plane, out_rows, :] = jnp.where(ok, fresh, 0.0)
        return carry

    lax.fori_loop(planes[0], planes[1], plane_body, 0)


def _down_kernel(off_ref, s_ref, u2_ref, r_ref, u1_ref, *, extent_x, extent_y):
    depth_x = s_ref.shape[1]
    common = dict(scale=1.0, extent_x=extent_x, extent_y=extent_y)
    _sweep_planes(off_ref, s_ref.at[0], s_ref.at[1], s_ref.at[2], u1_ref, residual=False,
                  planes=(1, depth_x - 1), inner=False, **common)
    _sweep_planes(off_ref, u1_ref, s_ref.at[1], s_ref.at[2], u2_ref, residual=False,
                  planes=(2, depth_x - 2), inner=False, **common)
    _sweep_planes(off_ref, u2_ref, s_ref.at[1], s_ref.at[2], r_ref, residual=True,
                  planes=(4, depth_x - 4), inner=True, **common)


def _up_kernel(off_ref, u2_ref, e_ref, s_ref, u5_ref, u3_ref, u4_ref, *, extent_x, extent_y):
    depth_x = s_ref.shape[1]
    common = dict(scale=1.0, extent_x=extent_x, extent_y=extent_y)

    def add_plane(p, carry):
        u3_ref[p] = u2_ref[p] + e_ref[p // 2 - 1]
        return carry

    lax.fori_loop(2, depth_x - 2, add_plane, 0)
    _sweep_planes(off_ref, u3_ref, s_ref.at[1], s_ref.at[2], u4_ref, residual=False,
                  planes=(3, depth_x - 3), inner=False, **common)
    _sweep_planes(off_ref, u4_ref, s_ref.at[1], s_ref.at[2], u5_ref, residual=False,
                  planes=(4, depth_x - 4), inner=True, **common)


def _frame_call(kernel, offsets, arrays, outs, scratch, cells, passes):
    vmem = pl.BlockSpec(memory_space=pltpu.VMEM)
    return pl.pallas_call(
        kernel,
        grid=(1,),
        out_shape=outs,
        in_specs=[pl.BlockSpec(memory_space=pltpu.SMEM)] + [vmem] * len(arrays),
        out_specs=[vmem] * len(outs) if isinstance(outs, (list, tuple)) else vmem,
        scratch_shapes=scratch,
        compiler_params=pltpu.CompilerParams(vmem_limit_bytes=60 * 1024 * 1024),
        cost_estimate=pl.CostEstimate(flops=40 * cells * passes, transcendentals=0,
                                      bytes_accessed=4 * 5 * cells),
    )(offsets, *arrays)


def on_device(start_field, source, conductance):
    nx, ny = start_field.shape[0], start_field.shape[1]
    mx, my = nx // 2, ny // 2
    lx, ly = nx // 4, ny // 4

    with jax.named_scope("level0_down"):
        fine = exchange(jnp.stack([start_field, source, conductance]), 4)
        extent_x, extent_y = nx * lax.axis_size("row"), ny * lax.axis_size("col")
        offsets = jnp.stack([lax.axis_index("row") * nx - 4, lax.axis_index("col") * ny - 4]).astype(jnp.int32)
        depth_x, depth_y, depth_z = fine.shape[1:]
        frame = jax.ShapeDtypeStruct((depth_x, depth_y, depth_z), jnp.float32)
        inner = jax.ShapeDtypeStruct((depth_x - 8, depth_y - 8, depth_z), jnp.float32)
        kernel = functools.partial(_down_kernel, extent_x=extent_x, extent_y=extent_y)
        u2, residual = _frame_call(kernel, offsets, [fine], [frame, inner],
                                   [pltpu.VMEM(frame.shape, jnp.float32)], fine[0].size, 3)
        mid_rhs = restrict_mean(residual)
        mid_cond = restrict_mean(conductance)

    with jax.named_scope("level1_down"):
        mid = exchange(jnp.stack([mid_rhs, mid_cond]), 4)
        rhs1, k1 = mid[0], mid[1]
        e1 = first_guess(trim(rhs1, 1), k1, 0.25, grid_mask(mx, my, 3))
        e1 = sweep(e1, trim(rhs1, 2), trim(k1, 1), 0.25, grid_mask(mx, my, 2))
        image = operate(trim(e1, 1), trim(k1, 3), 0.25)[0]
        low_rhs = restrict_mean(mid_rhs - image)
        low_cond = restrict_mean(mid_cond)

    with jax.named_scope("level2"):
        low = exchange(jnp.stack([low_rhs, low_cond]), 5)
        rhs2, k2 = low[0], low[1]
        e2 = first_guess(trim(rhs2, 1), k2, 0.0625, grid_mask(lx, ly, 4))
        for halo in (3, 2, 1):
            e2 = sweep(e2, trim(rhs2, 5 - halo), trim(k2, 4 - halo), 0.0625, grid_mask(lx, ly, halo))

    with jax.named_scope("level1_up"):
        e1 = e1 + prolong_copy(e2)
        e1 = sweep(e1, trim(rhs1, 3), trim(k1, 2), 0.25, grid_mask(mx, my, 1))

    with jax.named_scope("level0_up"):
        coarse_z = e1.shape[2]
        coarse_idx = lax.broadcasted_iota(jnp.int32, (coarse_z, 2 * coarse_z), 0)
        fine_idx = lax.broadcasted_iota(jnp.int32, (coarse_z, 2 * coarse_z), 1)
        table = jnp.where(fine_idx // 2 == coarse_idx, 1.0, 0.0).astype(jnp.float32)
        deeper = jnp.dot(e1, table, precision=lax.Precision.HIGHEST, preferred_element_type=jnp.float32)
        wider = jnp.pad(jnp.repeat(deeper, 2, 1), ((0, 0), (2, 2), (0, 0)))
        kernel = functools.partial(_up_kernel, extent_x=extent_x, extent_y=extent_y)
        u5 = _frame_call(kernel, offsets, [u2, wider, fine], inner,
                         [pltpu.VMEM(frame.shape, jnp.float32), pltpu.VMEM(frame.shape, jnp.float32)],
                         fine[0].size, 2)
    return u5


def solution(mesh):
    placed = (P("row", "col", None), P("row", "col", None), P("row", "col", None))
    return jax.shard_map(
        on_device, mesh=mesh, in_specs=placed, out_specs=P("row", "col", None), check_vma=False
    )
```

```python
import functools

import jax
import jax.numpy as jnp
from jax import lax
from jax.experimental import pallas as pl
from jax.experimental.pallas import tpu as pltpu
from jax.sharding import PartitionSpec as P

damping = 2.0 / 3.0


def _shift_pairs(axis, step):
    count = lax.axis_size(axis)
    return [(i, i + step) for i in range(count) if 0 <= i + step < count]


def exchange(arrays, width):
    w = width
    y_lo = lax.ppermute(jnp.stack([a[:, -w:] for a in arrays]), "col", _shift_pairs("col", 1))
    y_hi = lax.ppermute(jnp.stack([a[:, :w] for a in arrays]), "col", _shift_pairs("col", -1))
    first_x = jnp.concatenate([y_lo[:, :w], jnp.stack([a[:w] for a in arrays]), y_hi[:, :w]], axis=2)
    last_x = jnp.concatenate([y_lo[:, -w:], jnp.stack([a[-w:] for a in arrays]), y_hi[:, -w:]], axis=2)
    x_lo = lax.ppermute(last_x, "row", _shift_pairs("row", 1))
    x_hi = lax.ppermute(first_x, "row", _shift_pairs("row", -1))
    middle = jnp.concatenate([y_lo, jnp.stack(arrays), y_hi], axis=2)
    return jnp.concatenate([x_lo, middle, x_hi], axis=1)


def trim(field, k):
    if k == 0:
        return field
    return field[k:-k, k:-k]


def grid_mask(nx, ny, halo):
    rows = lax.axis_size("row")
    cols = lax.axis_size("col")
    gx = lax.axis_index("row") * nx - halo + lax.broadcasted_iota(jnp.int32, (nx + 2 * halo, 1, 1), 0)
    gy = lax.axis_index("col") * ny - halo + lax.broadcasted_iota(jnp.int32, (1, ny + 2 * halo, 1), 1)
    return ((gx >= 0) & (gx < nx * rows)) & ((gy >= 0) & (gy < ny * cols))


def z_lo(field):
    depth_idx = lax.broadcasted_iota(jnp.int32, field.shape, field.ndim - 1)
    return jnp.where(depth_idx == 0, 0.0, jnp.roll(field, 1, field.ndim - 1))


def z_hi(field):
    depth_idx = lax.broadcasted_iota(jnp.int32, field.shape, field.ndim - 1)
    return jnp.where(depth_idx == field.shape[-1] - 1, 0.0, jnp.roll(field, -1, field.ndim - 1))


def coefs(cond, scale):
    half = 0.5 * scale
    centre = cond[1:-1, 1:-1]
    wxm = (centre + cond[:-2, 1:-1]) * half
    wxp = (cond[2:, 1:-1] + centre) * half
    wym = (centre + cond[1:-1, :-2]) * half
    wyp = (cond[1:-1, 2:] + centre) * half
    wzm = (centre + z_lo(centre)) * half
    wzp = (z_hi(centre) + centre) * half
    diagonal = wxm + wxp + wym + wyp + wzm + wzp
    return wxm, wxp, wym, wyp, wzm, wzp, diagonal


def operate(field, cond, scale):
    wxm, wxp, wym, wyp, wzm, wzp, diagonal = coefs(cond, scale)
    centre = field[1:-1, 1:-1]
    beside = wxm * field[:-2, 1:-1] + wxp * field[2:, 1:-1]
    beside = beside + wym * field[1:-1, :-2] + wyp * field[1:-1, 2:]
    beside = beside + wzm * z_lo(centre) + wzp * z_hi(centre)
    return diagonal * centre - beside, diagonal, centre


def sweep(field, rhs, cond, scale, mask):
    image, diagonal, centre = operate(field, cond, scale)
    return jnp.where(mask, centre + damping * (rhs - image) / diagonal, 0.0)


def first_guess(rhs, cond, scale, mask):
    diagonal = coefs(cond, scale)[6]
    return jnp.where(mask, damping * rhs / diagonal, 0.0)


def restrict_mean(field):
    depth = field.shape[2]
    planar = field.reshape(field.shape[0] // 2, 2, field.shape[1] // 2, 2, depth).sum(axis=(1, 3))
    fine_idx = lax.broadcasted_iota(jnp.int32, (depth, depth // 2), 0)
    coarse_idx = lax.broadcasted_iota(jnp.int32, (depth, depth // 2), 1)
    table = jnp.where(fine_idx // 2 == coarse_idx, 0.125, 0.0).astype(jnp.float32)
    return jnp.dot(
        planar, table, precision=lax.Precision.HIGHEST, preferred_element_type=jnp.float32
    )


def prolong_copy(field):
    depth = field.shape[2]
    coarse_idx = lax.broadcasted_iota(jnp.int32, (depth, 2 * depth), 0)
    fine_idx = lax.broadcasted_iota(jnp.int32, (depth, 2 * depth), 1)
    table = jnp.where(fine_idx // 2 == coarse_idx, 1.0, 0.0).astype(jnp.float32)
    deeper = jnp.dot(
        field, table, precision=lax.Precision.HIGHEST, preferred_element_type=jnp.float32
    )
    return jnp.repeat(jnp.repeat(deeper, 2, 0), 2, 1)


CHUNK = 8


def _plane_kernel(off_ref, u_ref, ulo_ref, uhi_ref, b_ref, k_ref, klo_ref, khi_ref, o_ref, *,
                  scale, extent_x, extent_y, residual, chunk, inner):
    step = pl.program_id(0)
    depth_y, depth_z = u_ref.shape[-2], u_ref.shape[-1]
    first = 4 if inner else 0
    tiles = (depth_y - 2 * first) // 8
    half = 0.5 * scale
    z_idx = lax.broadcasted_iota(jnp.int32, (8, depth_z), 1)
    z_first = z_idx == 0
    z_last = z_idx == depth_z - 1
    row_idx = lax.broadcasted_iota(jnp.int32, (8, depth_z), 0)

    def z_lo(a):
        return jnp.where(z_first, 0.0, pltpu.roll(a, 1, 1))

    def z_hi(a):
        return jnp.where(z_last, 0.0, pltpu.roll(a, depth_z - 1, 1))

    def rows(ref, plane, t, shift):
        start = first + 8 * t
        if shift == 0:
            return ref[plane, pl.ds(start, 8), :]
        if shift < 0 and start == 0:
            return pltpu.roll(ref[plane, pl.ds(0, 8), :], 1, 0)
        if shift > 0 and start + 8 == depth_y:
            return pltpu.roll(ref[plane, pl.ds(start, 8), :], 7, 0)
        return ref[plane, pl.ds(start + shift, 8), :]

    for p in range(chunk):
        k_m = (klo_ref, 0) if p == 0 else (k_ref, p - 1)
        k_p = (khi_ref, 0) if p == chunk - 1 else (k_ref, p + 1)
        u_m = (ulo_ref, 0) if p == 0 else (u_ref, p - 1)
        u_p = (uhi_ref, 0) if p == chunk - 1 else (u_ref, p + 1)
        x_idx = off_ref[0] + first + step * chunk + p
        x_ok = (x_idx >= 0) & (x_idx < extent_x)
        for t in range(tiles):
            kc = rows(k_ref, p, t, 0)
            uc = rows(u_ref, p, t, 0)
            sxm = kc + rows(k_m[0], k_m[1], t, 0)
            sxp = rows(k_p[0], k_p[1], t, 0) + kc
            sym = kc + rows(k_ref, p, t, -1)
            syp = rows(k_ref, p, t, 1) + kc
            szm = kc + z_lo(kc)
            szp = z_hi(kc) + kc
            total = sxm + sxp + sym + syp + szm + szp
            beside = sxm * rows(u_m[0], u_m[1], t, 0) + sxp * rows(u_p[0], u_p[1], t, 0)
            beside = beside + sym * rows(u_ref, p, t, -1) + syp * rows(u_ref, p, t, 1)
            beside = beside + szm * z_lo(uc) + szp * z_hi(uc)
            image = (total * uc - beside) * half
            rhs = rows(b_ref, p, t, 0)
            out_rows = pl.ds(8 * t if inner else first + 8 * t, 8)
            if residual:
                o_ref[p, out_rows, :] = rhs - image
            else:
                y_idx = off_ref[1] + first + 8 * t + row_idx
                ok = x_ok & (y_idx >= 0) & (y_idx < extent_y)
                fresh = uc + damping * (rhs - image) / (total * half)
                o_ref[p, out_rows, :] = jnp.where(ok, fresh, 0.0)


def plane_step(offsets, u, b, k, scale, extent_x, extent_y, residual=False, inner=False):
    (u_arr, u_i), (b_arr, b_i), (k_arr, k_i) = u, b, k
    depth_x, depth_y, depth_z = u_arr.shape[-3:]
    chunk = 4 if inner else CHUNK
    lead_blocks = 1 if inner else 0
    chunks = (depth_x - 8 * lead_blocks) // chunk

    def spec(arr, idx, kind):
        lead = (None,) if arr.ndim == 4 else ()
        pre = (idx,) if arr.ndim == 4 else ()
        if kind == "main":
            return pl.BlockSpec(lead + (chunk, depth_y, depth_z),
                                lambda i, off: pre + (i + lead_blocks, 0, 0))
        if kind == "lo":
            return pl.BlockSpec(lead + (1, depth_y, depth_z),
                                lambda i, off: pre + (jnp.maximum((i + lead_blocks) * chunk - 1, 0), 0, 0))
        return pl.BlockSpec(lead + (1, depth_y, depth_z),
                            lambda i, off: pre + (jnp.minimum((i + lead_blocks) * chunk + chunk, depth_x - 1), 0, 0))

    kernel = functools.partial(_plane_kernel, scale=scale, extent_x=extent_x, extent_y=extent_y,
                               residual=residual, chunk=chunk, inner=inner)
    out_x = depth_x - 8 if inner else depth_x
    out_y = depth_y - 8 if inner else depth_y
    grid_spec = pltpu.PrefetchScalarGridSpec(
        num_scalar_prefetch=1,
        grid=(chunks,),
        in_specs=[spec(u_arr, u_i, "main"), spec(u_arr, u_i, "lo"), spec(u_arr, u_i, "hi"),
                  spec(b_arr, b_i, "main"),
                  spec(k_arr, k_i, "main"), spec(k_arr, k_i, "lo"), spec(k_arr, k_i, "hi")],
        out_specs=pl.BlockSpec((chunk, out_y, depth_z), lambda i, off: (i, 0, 0)),
    )
    cells = out_x * out_y * depth_z
    return pl.pallas_call(
        kernel,
        grid_spec=grid_spec,
        out_shape=jax.ShapeDtypeStruct((out_x, out_y, depth_z), jnp.float32),
        compiler_params=pltpu.CompilerParams(dimension_semantics=("arbitrary",)),
        cost_estimate=pl.CostEstimate(flops=45 * cells, transcendentals=0, bytes_accessed=4 * 4 * cells),
    )(offsets, u_arr, u_arr, u_arr, b_arr, k_arr, k_arr, k_arr)


def _sweep_planes(off_ref, u_ref, b_ref, k_ref, o_ref, *, scale, extent_x, extent_y, residual,
                  planes, inner):
    depth_y, depth_z = u_ref.shape[-2], u_ref.shape[-1]
    first = 4 if inner else 0
    tiles = (depth_y - 2 * first) // 8
    half = 0.5 * scale
    z_idx = lax.broadcasted_iota(jnp.int32, (8, depth_z), 1)
    z_first = z_idx == 0
    z_last = z_idx == depth_z - 1
    row_idx = lax.broadcasted_iota(jnp.int32, (8, depth_z), 0)

    def z_lo(a):
        return jnp.where(z_first, 0.0, pltpu.roll(a, 1, 1))

    def z_hi(a):
        return jnp.where(z_last, 0.0, pltpu.roll(a, depth_z - 1, 1))

    def rows(ref, plane, t, shift):
        start = first + 8 * t
        if shift == 0:
            return ref[plane, pl.ds(start, 8), :]
        if shift < 0 and start == 0:
            return pltpu.roll(ref[plane, pl.ds(0, 8), :], 1, 0)
        if shift > 0 and start + 8 == depth_y:
            return pltpu.roll(ref[plane, pl.ds(start, 8), :], 7, 0)
        return ref[plane, pl.ds(start + shift, 8), :]

    def plane_body(p, carry):
        x_idx = off_ref[0] + p
        x_ok = (x_idx >= 0) & (x_idx < extent_x)
        out_plane = p - first
        for t in range(tiles):
            kc = rows(k_ref, p, t, 0)
            uc = rows(u_ref, p, t, 0)
            sxm = kc + rows(k_ref, p - 1, t, 0)
            sxp = rows(k_ref, p + 1, t, 0) + kc
            sym = kc + rows(k_ref, p, t, -1)
            syp = rows(k_ref, p, t, 1) + kc
            szm = kc + z_lo(kc)
            szp = z_hi(kc) + kc
            total = sxm + sxp + sym + syp + szm + szp
            beside = sxm * rows(u_ref, p - 1, t, 0) + sxp * rows(u_ref, p + 1, t, 0)
            beside = beside + sym * rows(u_ref, p, t, -1) + syp * rows(u_ref, p, t, 1)
            beside = beside + szm * z_lo(uc) + szp * z_hi(uc)
            image = (total * uc - beside) * half
            rhs = rows(b_ref, p, t, 0)
            out_rows = pl.ds(8 * t if inner else first + 8 * t, 8)
            if residual:
                o_ref[out_plane, out_rows, :] = rhs - image
            else:
                y_idx = off_ref[1] + first + 8 * t + row_idx
                ok = x_ok & (y_idx >= 0) & (y_idx < extent_y)
                fresh = uc + damping * (rhs - image) / (total * half)
                o_ref[out_plane, out_rows, :] = jnp.where(ok, fresh, 0.0)
        return carry

    lax.fori_loop(planes[0], planes[1], plane_body, 0)


def _down_kernel(off_ref, s_ref, u2_ref, r_ref, u1_ref, *, extent_x, extent_y):
    depth_x = s_ref.shape[1]
    common = dict(scale=1.0, extent_x=extent_x, extent_y=extent_y)
    _sweep_planes(off_ref, s_ref.at[0], s_ref.at[1], s_ref.at[2], u1_ref, residual=False,
                  planes=(1, depth_x - 1), inner=False, **common)
    _sweep_planes(off_ref, u1_ref, s_ref.at[1], s_ref.at[2], u2_ref, residual=False,
                  planes=(2, depth_x - 2), inner=False, **common)
    _sweep_planes(off_ref, u2_ref, s_ref.at[1], s_ref.at[2], r_ref, residual=True,
                  planes=(4, depth_x - 4), inner=True, **common)


def _up_kernel(off_ref, u2_ref, e_ref, s_ref, u5_ref, u3_ref, u4_ref, *, extent_x, extent_y):
    depth_x = s_ref.shape[1]
    common = dict(scale=1.0, extent_x=extent_x, extent_y=extent_y)

    def add_plane(p, carry):
        u3_ref[p] = u2_ref[p] + e_ref[p // 2 - 1]
        return carry

    lax.fori_loop(2, depth_x - 2, add_plane, 0)
    _sweep_planes(off_ref, u3_ref, s_ref.at[1], s_ref.at[2], u4_ref, residual=False,
                  planes=(3, depth_x - 3), inner=False, **common)
    _sweep_planes(off_ref, u4_ref, s_ref.at[1], s_ref.at[2], u5_ref, residual=False,
                  planes=(4, depth_x - 4), inner=True, **common)


def _frame_call(kernel, offsets, arrays, outs, scratch, cells, passes):
    vmem = pl.BlockSpec(memory_space=pltpu.VMEM)
    return pl.pallas_call(
        kernel,
        grid=(1,),
        out_shape=outs,
        in_specs=[pl.BlockSpec(memory_space=pltpu.SMEM)] + [vmem] * len(arrays),
        out_specs=[vmem] * len(outs) if isinstance(outs, (list, tuple)) else vmem,
        scratch_shapes=scratch,
        compiler_params=pltpu.CompilerParams(vmem_limit_bytes=60 * 1024 * 1024),
        cost_estimate=pl.CostEstimate(flops=40 * cells * passes, transcendentals=0,
                                      bytes_accessed=4 * 5 * cells),
    )(offsets, *arrays)


def on_device(start_field, source, conductance):
    nx, ny = start_field.shape[0], start_field.shape[1]
    mx, my = nx // 2, ny // 2
    lx, ly = nx // 4, ny // 4

    with jax.named_scope("level0_down"):
        fine = exchange([start_field, source, conductance], 4)
        extent_x, extent_y = nx * lax.axis_size("row"), ny * lax.axis_size("col")
        offsets = jnp.stack([lax.axis_index("row") * nx - 4, lax.axis_index("col") * ny - 4]).astype(jnp.int32)
        depth_x, depth_y, depth_z = fine.shape[1:]
        frame = jax.ShapeDtypeStruct((depth_x, depth_y, depth_z), jnp.float32)
        inner = jax.ShapeDtypeStruct((depth_x - 8, depth_y - 8, depth_z), jnp.float32)
        kernel = functools.partial(_down_kernel, extent_x=extent_x, extent_y=extent_y)
        u2, residual = _frame_call(kernel, offsets, [fine], [frame, inner],
                                   [pltpu.VMEM(frame.shape, jnp.float32)], fine[0].size, 3)
        mid_rhs = restrict_mean(residual)
        mid_cond = restrict_mean(conductance)

    with jax.named_scope("level1_down"):
        mid = exchange([mid_rhs, mid_cond], 4)
        rhs1, k1 = mid[0], mid[1]
        e1 = first_guess(trim(rhs1, 1), k1, 0.25, grid_mask(mx, my, 3))
        e1 = sweep(e1, trim(rhs1, 2), trim(k1, 1), 0.25, grid_mask(mx, my, 2))
        image = operate(trim(e1, 1), trim(k1, 3), 0.25)[0]
        low_rhs = restrict_mean(mid_rhs - image)
        low_cond = restrict_mean(mid_cond)

    with jax.named_scope("level2"):
        low = exchange([low_rhs, low_cond], 5)
        rhs2, k2 = low[0], low[1]
        e2 = first_guess(trim(rhs2, 1), k2, 0.0625, grid_mask(lx, ly, 4))
        for halo in (3, 2, 1):
            e2 = sweep(e2, trim(rhs2, 5 - halo), trim(k2, 4 - halo), 0.0625, grid_mask(lx, ly, halo))

    with jax.named_scope("level1_up"):
        e1 = e1 + prolong_copy(e2)
        e1 = sweep(e1, trim(rhs1, 3), trim(k1, 2), 0.25, grid_mask(mx, my, 1))

    with jax.named_scope("level0_up"):
        coarse_z = e1.shape[2]
        coarse_idx = lax.broadcasted_iota(jnp.int32, (coarse_z, 2 * coarse_z), 0)
        fine_idx = lax.broadcasted_iota(jnp.int32, (coarse_z, 2 * coarse_z), 1)
        table = jnp.where(fine_idx // 2 == coarse_idx, 1.0, 0.0).astype(jnp.float32)
        deeper = jnp.dot(e1, table, precision=lax.Precision.HIGHEST, preferred_element_type=jnp.float32)
        wider = jnp.pad(jnp.repeat(deeper, 2, 1), ((0, 0), (2, 2), (0, 0)))
        kernel = functools.partial(_up_kernel, extent_x=extent_x, extent_y=extent_y)
        u5 = _frame_call(kernel, offsets, [u2, wider, fine], inner,
                         [pltpu.VMEM(frame.shape, jnp.float32), pltpu.VMEM(frame.shape, jnp.float32)],
                         fine[0].size, 2)
    return u5


def solution(mesh):
    placed = (P("row", "col", None), P("row", "col", None), P("row", "col", None))
    return jax.shard_map(
        on_device, mesh=mesh, in_specs=placed, out_specs=P("row", "col", None), check_vma=False
    )
```

```python
import functools

import jax
import jax.numpy as jnp
from jax import lax
from jax.experimental import pallas as pl
from jax.experimental.pallas import tpu as pltpu
from jax.sharding import PartitionSpec as P

damping = 2.0 / 3.0


def exchange(stack, width):
    for axis, dim in (("col", 2), ("row", 1)):
        count = lax.axis_size(axis)
        forward = [(i, i + 1) for i in range(count - 1)]
        backward = [(i + 1, i) for i in range(count - 1)]
        size = stack.shape[dim]
        low = lax.ppermute(lax.slice_in_dim(stack, size - width, size, axis=dim), axis, forward)
        high = lax.ppermute(lax.slice_in_dim(stack, 0, width, axis=dim), axis, backward)
        stack = jnp.concatenate([low, stack, high], axis=dim)
    return stack


def trim(field, k):
    if k == 0:
        return field
    return field[k:-k, k:-k]


def grid_mask(nx, ny, halo):
    rows = lax.axis_size("row")
    cols = lax.axis_size("col")
    gx = lax.axis_index("row") * nx - halo + lax.broadcasted_iota(jnp.int32, (nx + 2 * halo, 1, 1), 0)
    gy = lax.axis_index("col") * ny - halo + lax.broadcasted_iota(jnp.int32, (1, ny + 2 * halo, 1), 1)
    return ((gx >= 0) & (gx < nx * rows)) & ((gy >= 0) & (gy < ny * cols))


def z_lo(field):
    depth_idx = lax.broadcasted_iota(jnp.int32, field.shape, field.ndim - 1)
    return jnp.where(depth_idx == 0, 0.0, jnp.roll(field, 1, field.ndim - 1))


def z_hi(field):
    depth_idx = lax.broadcasted_iota(jnp.int32, field.shape, field.ndim - 1)
    return jnp.where(depth_idx == field.shape[-1] - 1, 0.0, jnp.roll(field, -1, field.ndim - 1))


def coefs(cond, scale):
    half = 0.5 * scale
    centre = cond[1:-1, 1:-1]
    wxm = (centre + cond[:-2, 1:-1]) * half
    wxp = (cond[2:, 1:-1] + centre) * half
    wym = (centre + cond[1:-1, :-2]) * half
    wyp = (cond[1:-1, 2:] + centre) * half
    wzm = (centre + z_lo(centre)) * half
    wzp = (z_hi(centre) + centre) * half
    diagonal = wxm + wxp + wym + wyp + wzm + wzp
    return wxm, wxp, wym, wyp, wzm, wzp, diagonal


def operate(field, cond, scale):
    wxm, wxp, wym, wyp, wzm, wzp, diagonal = coefs(cond, scale)
    centre = field[1:-1, 1:-1]
    beside = wxm * field[:-2, 1:-1] + wxp * field[2:, 1:-1]
    beside = beside + wym * field[1:-1, :-2] + wyp * field[1:-1, 2:]
    beside = beside + wzm * z_lo(centre) + wzp * z_hi(centre)
    return diagonal * centre - beside, diagonal, centre


def sweep(field, rhs, cond, scale, mask):
    image, diagonal, centre = operate(field, cond, scale)
    return jnp.where(mask, centre + damping * (rhs - image) / diagonal, 0.0)


def first_guess(rhs, cond, scale, mask):
    diagonal = coefs(cond, scale)[6]
    return jnp.where(mask, damping * rhs / diagonal, 0.0)


def restrict_mean(field):
    depth = field.shape[2]
    planar = field.reshape(field.shape[0] // 2, 2, field.shape[1] // 2, 2, depth).sum(axis=(1, 3))
    fine_idx = lax.broadcasted_iota(jnp.int32, (depth, depth // 2), 0)
    coarse_idx = lax.broadcasted_iota(jnp.int32, (depth, depth // 2), 1)
    table = jnp.where(fine_idx // 2 == coarse_idx, 0.125, 0.0).astype(jnp.float32)
    return jnp.dot(
        planar, table, precision=lax.Precision.HIGHEST, preferred_element_type=jnp.float32
    )


def restrict_pairs(field):
    depth = field.shape[2]
    planar = field.reshape(field.shape[0], field.shape[1] // 2, 2, depth).sum(axis=2)
    fine_idx = lax.broadcasted_iota(jnp.int32, (depth, depth // 2), 0)
    coarse_idx = lax.broadcasted_iota(jnp.int32, (depth, depth // 2), 1)
    table = jnp.where(fine_idx // 2 == coarse_idx, 0.125, 0.0).astype(jnp.float32)
    return jnp.dot(
        planar, table, precision=lax.Precision.HIGHEST, preferred_element_type=jnp.float32
    )


def prolong_copy(field):
    depth = field.shape[2]
    coarse_idx = lax.broadcasted_iota(jnp.int32, (depth, 2 * depth), 0)
    fine_idx = lax.broadcasted_iota(jnp.int32, (depth, 2 * depth), 1)
    table = jnp.where(fine_idx // 2 == coarse_idx, 1.0, 0.0).astype(jnp.float32)
    deeper = jnp.dot(
        field, table, precision=lax.Precision.HIGHEST, preferred_element_type=jnp.float32
    )
    return jnp.repeat(jnp.repeat(deeper, 2, 0), 2, 1)


CHUNK = 8


def _plane_kernel(off_ref, u_ref, ulo_ref, uhi_ref, b_ref, k_ref, klo_ref, khi_ref, o_ref, *,
                  scale, extent_x, extent_y, residual, chunk, inner):
    step = pl.program_id(0)
    depth_y, depth_z = u_ref.shape[-2], u_ref.shape[-1]
    first = 4 if inner else 0
    tiles = (depth_y - 2 * first) // 8
    half = 0.5 * scale
    z_idx = lax.broadcasted_iota(jnp.int32, (8, depth_z), 1)
    z_first = z_idx == 0
    z_last = z_idx == depth_z - 1
    row_idx = lax.broadcasted_iota(jnp.int32, (8, depth_z), 0)

    def z_lo(a):
        return jnp.where(z_first, 0.0, pltpu.roll(a, 1, 1))

    def z_hi(a):
        return jnp.where(z_last, 0.0, pltpu.roll(a, depth_z - 1, 1))

    def rows(ref, plane, t, shift):
        start = first + 8 * t
        if shift == 0:
            return ref[plane, pl.ds(start, 8), :]
        if shift < 0 and start == 0:
            return pltpu.roll(ref[plane, pl.ds(0, 8), :], 1, 0)
        if shift > 0 and start + 8 == depth_y:
            return pltpu.roll(ref[plane, pl.ds(start, 8), :], 7, 0)
        return ref[plane, pl.ds(start + shift, 8), :]

    for p in range(chunk):
        k_m = (klo_ref, 0) if p == 0 else (k_ref, p - 1)
        k_p = (khi_ref, 0) if p == chunk - 1 else (k_ref, p + 1)
        u_m = (ulo_ref, 0) if p == 0 else (u_ref, p - 1)
        u_p = (uhi_ref, 0) if p == chunk - 1 else (u_ref, p + 1)
        x_idx = off_ref[0] + first + step * chunk + p
        x_ok = (x_idx >= 0) & (x_idx < extent_x)
        for t in range(tiles):
            kc = rows(k_ref, p, t, 0)
            uc = rows(u_ref, p, t, 0)
            sxm = kc + rows(k_m[0], k_m[1], t, 0)
            sxp = rows(k_p[0], k_p[1], t, 0) + kc
            sym = kc + rows(k_ref, p, t, -1)
            syp = rows(k_ref, p, t, 1) + kc
            szm = kc + z_lo(kc)
            szp = z_hi(kc) + kc
            total = sxm + sxp + sym + syp + szm + szp
            beside = sxm * rows(u_m[0], u_m[1], t, 0) + sxp * rows(u_p[0], u_p[1], t, 0)
            beside = beside + sym * rows(u_ref, p, t, -1) + syp * rows(u_ref, p, t, 1)
            beside = beside + szm * z_lo(uc) + szp * z_hi(uc)
            image = (total * uc - beside) * half
            rhs = rows(b_ref, p, t, 0)
            out_rows = pl.ds(8 * t if inner else first + 8 * t, 8)
            if residual:
                o_ref[p, out_rows, :] = rhs - image
            else:
                y_idx = off_ref[1] + first + 8 * t + row_idx
                ok = x_ok & (y_idx >= 0) & (y_idx < extent_y)
                fresh = uc + damping * (rhs - image) / (total * half)
                o_ref[p, out_rows, :] = jnp.where(ok, fresh, 0.0)


def plane_step(offsets, u, b, k, scale, extent_x, extent_y, residual=False, inner=False):
    (u_arr, u_i), (b_arr, b_i), (k_arr, k_i) = u, b, k
    depth_x, depth_y, depth_z = u_arr.shape[-3:]
    chunk = 4 if inner else CHUNK
    lead_blocks = 1 if inner else 0
    chunks = (depth_x - 8 * lead_blocks) // chunk

    def spec(arr, idx, kind):
        lead = (None,) if arr.ndim == 4 else ()
        pre = (idx,) if arr.ndim == 4 else ()
        if kind == "main":
            return pl.BlockSpec(lead + (chunk, depth_y, depth_z),
                                lambda i, off: pre + (i + lead_blocks, 0, 0))
        if kind == "lo":
            return pl.BlockSpec(lead + (1, depth_y, depth_z),
                                lambda i, off: pre + (jnp.maximum((i + lead_blocks) * chunk - 1, 0), 0, 0))
        return pl.BlockSpec(lead + (1, depth_y, depth_z),
                            lambda i, off: pre + (jnp.minimum((i + lead_blocks) * chunk + chunk, depth_x - 1), 0, 0))

    kernel = functools.partial(_plane_kernel, scale=scale, extent_x=extent_x, extent_y=extent_y,
                               residual=residual, chunk=chunk, inner=inner)
    out_x = depth_x - 8 if inner else depth_x
    out_y = depth_y - 8 if inner else depth_y
    grid_spec = pltpu.PrefetchScalarGridSpec(
        num_scalar_prefetch=1,
        grid=(chunks,),
        in_specs=[spec(u_arr, u_i, "main"), spec(u_arr, u_i, "lo"), spec(u_arr, u_i, "hi"),
                  spec(b_arr, b_i, "main"),
                  spec(k_arr, k_i, "main"), spec(k_arr, k_i, "lo"), spec(k_arr, k_i, "hi")],
        out_specs=pl.BlockSpec((chunk, out_y, depth_z), lambda i, off: (i, 0, 0)),
    )
    cells = out_x * out_y * depth_z
    return pl.pallas_call(
        kernel,
        grid_spec=grid_spec,
        out_shape=jax.ShapeDtypeStruct((out_x, out_y, depth_z), jnp.float32),
        compiler_params=pltpu.CompilerParams(dimension_semantics=("arbitrary",)),
        cost_estimate=pl.CostEstimate(flops=45 * cells, transcendentals=0, bytes_accessed=4 * 4 * cells),
    )(offsets, u_arr, u_arr, u_arr, b_arr, k_arr, k_arr, k_arr)


def _sweep_planes(off_ref, u_ref, b_ref, k_ref, o_ref, *, scale, extent_x, extent_y, residual,
                  planes, inner):
    depth_y, depth_z = u_ref.shape[-2], u_ref.shape[-1]
    first = 4 if inner else 0
    tiles = (depth_y - 2 * first) // 8
    half = 0.5 * scale
    z_idx = lax.broadcasted_iota(jnp.int32, (8, depth_z), 1)
    z_first = z_idx == 0
    z_last = z_idx == depth_z - 1
    row_idx = lax.broadcasted_iota(jnp.int32, (8, depth_z), 0)

    def z_lo(a):
        return jnp.where(z_first, 0.0, pltpu.roll(a, 1, 1))

    def z_hi(a):
        return jnp.where(z_last, 0.0, pltpu.roll(a, depth_z - 1, 1))

    def rows(ref, plane, t, shift):
        start = first + 8 * t
        if shift == 0:
            return ref[plane, pl.ds(start, 8), :]
        if shift < 0 and start == 0:
            return pltpu.roll(ref[plane, pl.ds(0, 8), :], 1, 0)
        if shift > 0 and start + 8 == depth_y:
            return pltpu.roll(ref[plane, pl.ds(start, 8), :], 7, 0)
        return ref[plane, pl.ds(start + shift, 8), :]

    def plane_body(p, carry):
        x_idx = off_ref[0] + p
        x_ok = (x_idx >= 0) & (x_idx < extent_x)
        out_plane = p - first
        for t in range(tiles):
            kc = rows(k_ref, p, t, 0)
            uc = rows(u_ref, p, t, 0)
            sxm = kc + rows(k_ref, p - 1, t, 0)
            sxp = rows(k_ref, p + 1, t, 0) + kc
            sym = kc + rows(k_ref, p, t, -1)
            syp = rows(k_ref, p, t, 1) + kc
            szm = kc + z_lo(kc)
            szp = z_hi(kc) + kc
            total = sxm + sxp + sym + syp + szm + szp
            beside = sxm * rows(u_ref, p - 1, t, 0) + sxp * rows(u_ref, p + 1, t, 0)
            beside = beside + sym * rows(u_ref, p, t, -1) + syp * rows(u_ref, p, t, 1)
            beside = beside + szm * z_lo(uc) + szp * z_hi(uc)
            image = (total * uc - beside) * half
            rhs = rows(b_ref, p, t, 0)
            out_rows = pl.ds(8 * t if inner else first + 8 * t, 8)
            if residual:
                o_ref[out_plane, out_rows, :] = rhs - image
            else:
                y_idx = off_ref[1] + first + 8 * t + row_idx
                ok = x_ok & (y_idx >= 0) & (y_idx < extent_y)
                fresh = uc + damping * (rhs - image) / (total * half)
                o_ref[out_plane, out_rows, :] = jnp.where(ok, fresh, 0.0)
        return carry

    lax.fori_loop(planes[0], planes[1], plane_body, 0)


def _down_kernel(off_ref, s_ref, u2_ref, pairs_ref, u1_ref, r_ref, *, extent_x, extent_y):
    depth_x = s_ref.shape[1]
    common = dict(scale=1.0, extent_x=extent_x, extent_y=extent_y)
    _sweep_planes(off_ref, s_ref.at[0], s_ref.at[1], s_ref.at[2], u1_ref, residual=False,
                  planes=(1, depth_x - 1), inner=False, **common)
    _sweep_planes(off_ref, u1_ref, s_ref.at[1], s_ref.at[2], u2_ref, residual=False,
                  planes=(2, depth_x - 2), inner=False, **common)
    _sweep_planes(off_ref, u2_ref, s_ref.at[1], s_ref.at[2], r_ref, residual=True,
                  planes=(4, depth_x - 4), inner=True, **common)

    def add_pair(q, carry):
        pairs_ref[q] = r_ref[2 * q] + r_ref[2 * q + 1]
        return carry

    lax.fori_loop(0, pairs_ref.shape[0], add_pair, 0)


def _up_kernel(off_ref, u2_ref, e_ref, s_ref, u5_ref, u3_ref, u4_ref, *, extent_x, extent_y):
    depth_x = s_ref.shape[1]
    common = dict(scale=1.0, extent_x=extent_x, extent_y=extent_y)

    def add_plane(p, carry):
        u3_ref[p] = u2_ref[p] + e_ref[p // 2 - 1]
        return carry

    lax.fori_loop(2, depth_x - 2, add_plane, 0)
    _sweep_planes(off_ref, u3_ref, s_ref.at[1], s_ref.at[2], u4_ref, residual=False,
                  planes=(3, depth_x - 3), inner=False, **common)
    _sweep_planes(off_ref, u4_ref, s_ref.at[1], s_ref.at[2], u5_ref, residual=False,
                  planes=(4, depth_x - 4), inner=True, **common)


def _frame_call(kernel, offsets, arrays, outs, scratch, cells, passes):
    vmem = pl.BlockSpec(memory_space=pltpu.VMEM)
    return pl.pallas_call(
        kernel,
        grid=(1,),
        out_shape=outs,
        in_specs=[pl.BlockSpec(memory_space=pltpu.SMEM)] + [vmem] * len(arrays),
        out_specs=[vmem] * len(outs) if isinstance(outs, (list, tuple)) else vmem,
        scratch_shapes=scratch,
        compiler_params=pltpu.CompilerParams(vmem_limit_bytes=60 * 1024 * 1024),
        cost_estimate=pl.CostEstimate(flops=40 * cells * passes, transcendentals=0,
                                      bytes_accessed=4 * 5 * cells),
    )(offsets, *arrays)


def on_device(start_field, source, conductance):
    nx, ny = start_field.shape[0], start_field.shape[1]
    mx, my = nx // 2, ny // 2
    lx, ly = nx // 4, ny // 4

    with jax.named_scope("level0_down"):
        fine = exchange(jnp.stack([start_field, source, conductance]), 4)
        extent_x, extent_y = nx * lax.axis_size("row"), ny * lax.axis_size("col")
        offsets = jnp.stack([lax.axis_index("row") * nx - 4, lax.axis_index("col") * ny - 4]).astype(jnp.int32)
        depth_x, depth_y, depth_z = fine.shape[1:]
        frame = jax.ShapeDtypeStruct((depth_x, depth_y, depth_z), jnp.float32)
        inner = jax.ShapeDtypeStruct((depth_x - 8, depth_y - 8, depth_z), jnp.float32)
        paired = jax.ShapeDtypeStruct(((depth_x - 8) // 2, depth_y - 8, depth_z), jnp.float32)
        kernel = functools.partial(_down_kernel, extent_x=extent_x, extent_y=extent_y)
        u2, x_pairs = _frame_call(kernel, offsets, [fine], [frame, paired],
                                  [pltpu.VMEM(frame.shape, jnp.float32), pltpu.VMEM(inner.shape, jnp.float32)],
                                  fine[0].size, 3)
        mid_rhs = restrict_pairs(x_pairs)
        mid_cond = restrict_mean(conductance)

    with jax.named_scope("level1_down"):
        mid = exchange(jnp.stack([mid_rhs, mid_cond]), 4)
        rhs1, k1 = mid[0], mid[1]
        e1 = first_guess(trim(rhs1, 1), k1, 0.25, grid_mask(mx, my, 3))
        e1 = sweep(e1, trim(rhs1, 2), trim(k1, 1), 0.25, grid_mask(mx, my, 2))
        image = operate(trim(e1, 1), trim(k1, 3), 0.25)[0]
        low_rhs = restrict_mean(mid_rhs - image)
        low_cond = restrict_mean(mid_cond)

    with jax.named_scope("level2"):
        low = exchange(jnp.stack([low_rhs, low_cond]), 5)
        rhs2, k2 = low[0], low[1]
        e2 = first_guess(trim(rhs2, 1), k2, 0.0625, grid_mask(lx, ly, 4))
        for halo in (3, 2, 1):
            e2 = sweep(e2, trim(rhs2, 5 - halo), trim(k2, 4 - halo), 0.0625, grid_mask(lx, ly, halo))

    with jax.named_scope("level1_up"):
        e1 = e1 + prolong_copy(e2)
        e1 = sweep(e1, trim(rhs1, 3), trim(k1, 2), 0.25, grid_mask(mx, my, 1))

    with jax.named_scope("level0_up"):
        coarse_z = e1.shape[2]
        coarse_idx = lax.broadcasted_iota(jnp.int32, (coarse_z, 2 * coarse_z), 0)
        fine_idx = lax.broadcasted_iota(jnp.int32, (coarse_z, 2 * coarse_z), 1)
        table = jnp.where(fine_idx // 2 == coarse_idx, 1.0, 0.0).astype(jnp.float32)
        deeper = jnp.dot(e1, table, precision=lax.Precision.HIGHEST, preferred_element_type=jnp.float32)
        wider = jnp.pad(jnp.repeat(deeper, 2, 1), ((0, 0), (2, 2), (0, 0)))
        kernel = functools.partial(_up_kernel, extent_x=extent_x, extent_y=extent_y)
        u5 = _frame_call(kernel, offsets, [u2, wider, fine], inner,
                         [pltpu.VMEM(frame.shape, jnp.float32), pltpu.VMEM(frame.shape, jnp.float32)],
                         fine[0].size, 2)
    return u5


def solution(mesh):
    placed = (P("row", "col", None), P("row", "col", None), P("row", "col", None))
    return jax.shard_map(
        on_device, mesh=mesh, in_specs=placed, out_specs=P("row", "col", None), check_vma=False
    )
```
